256 devices in a mesh: dom: 64 (over y, z, core), rep: 4 (over x).
Axes of the slice: x: 4, y: 4, z: 8, core: 2. Of those that a mesh axis runs over, the one named last changes fastest.
Arguments:
- x_loader: bfloat16 [131072, 512], P(('dom', 'rep')), may hold values from -6 to 6
- owner_index: int32 [131072], P(('dom', 'rep')), may hold values from 0 to 131071, as said below
- tile_vals: bfloat16 [1024, 12, 128, 128], P(('dom', 'rep')), as said below
- tile_cols: int32 [1024, 12], P(('dom', 'rep')), may hold values from 0 to 1023, as said below
- tile_live: int32 [1024, 12], P(('dom', 'rep')), may hold values from 0 to 1, as said below
- w_self: bfloat16 [512, 512], replicated, may hold values from -0.25 to 0.25
- w_neigh: bfloat16 [512, 512], replicated, may hold values from -3 to 3
- bias: float32 [512], replicated, may hold values from -3 to 3
- cotangent: bfloat16 [131072, 512], P(('dom', 'rep')), may hold values from -6 to 6
Outputs:
- layer_out: bfloat16 [131072, 512], P(('dom', 'rep'))
- grad_features: bfloat16 [131072, 512], P(('dom', 'rep'))
- grad_self: float32 [512, 512], replicated
- grad_neigh: float32 [512, 512], replicated
- grad_bias: float32 [512], replicated
The draws below stay inside these ranges and needn't reach their ends.
Inputs may be any that keep to these rules, and one draw needn't show every extreme that they name: `owner_index`: A permutation of the 131072 rows. Loader rows are in blocks of 512 in the order of the devices (dom slowest); owner rows likewise. The 512 rows of each loader block with rep index r go to owner blocks of rep index r, 8 rows to each of the 64 partitions. `tile_cols`: partition p holds row tiles p * 16 to (p + 1) * 16 - 1. A column tile of a row tile of partition p lies in partition p or within 4 tiles beyond its edges. W is symmetric: every live slot (t, c) with tiles B is matched by a live slot (c, t) with tiles B^T, a slot with c = t holding a symmetric tile. `tile_live`: live slots are symmetric as stated for tile_cols. `tile_vals`: nonnegative edge weights.
All inputs are finite; a program needn't handle non-finite values.
Results may differ from the reference program's by a relative error of at most 0.0075.
Values may be sent and summed in bfloat16 or wider, within the bound.
No kernel may reach another device: no remote copies, remote signals or barrier semaphores. Data moves between devices by JAX's collectives and lax.ppermute only.
A program may use at most 64 MiB of HBM per device.

```python
import jax
import jax.numpy as jnp
from jax import lax

F = 512
RD = 512
K = 12
HALO_T = 4
NPART = 64
REPS = 4
PT = 16
V = 131072
NT = 1024
SENDS = 8


def permute_many(key, count, length):
    return jax.vmap(lambda sub: jax.random.permutation(sub, length))(jax.random.split(key, count))


def draw_owner_index(key, part):
    first_key = jax.random.fold_in(key, 11)
    second_key = jax.random.fold_in(key, 12)
    slot_perm = permute_many(first_key, REPS * NPART, RD).reshape(REPS, NPART, NPART, SENDS)
    slot_grid = jnp.transpose(slot_perm, (0, 2, 1, 3))
    dest_part = jnp.arange(NPART, dtype=jnp.int32)[None, None, :, None]
    rep_ids = jnp.arange(REPS, dtype=jnp.int32)[:, None, None, None]
    owner = dest_part * (RD * REPS) + rep_ids * RD + slot_grid.astype(jnp.int32)
    owner = owner.reshape(REPS, NPART, RD)
    shuffle = permute_many(second_key, REPS * NPART, RD).reshape(REPS, NPART, RD)
    owner = jnp.take_along_axis(owner, shuffle, axis=2)
    return jnp.transpose(owner, (1, 0, 2)).reshape(NPART * REPS * RD).astype(jnp.int32)


def intra_partners(key):
    perms = permute_many(key, NPART, PT).astype(jnp.int32)
    inverse = jnp.argsort(perms, axis=1).astype(jnp.int32)
    partner_pos = jnp.take_along_axis(perms, inverse ^ 1, axis=1)
    return (jnp.arange(NPART, dtype=jnp.int32)[:, None] * PT + partner_pos).reshape(NT)


def cross_partners(key):
    border = permute_many(jax.random.fold_in(key, 1), NPART, HALO_T).astype(jnp.int32)
    border_inv = jnp.argsort(border, axis=1).astype(jnp.int32)
    middle_len = PT - 2 * HALO_T
    middle = permute_many(jax.random.fold_in(key, 2), NPART, middle_len).astype(jnp.int32)
    middle_inv = jnp.argsort(middle, axis=1).astype(jnp.int32)
    pos = jnp.arange(PT, dtype=jnp.int32)
    parts = jnp.arange(NPART, dtype=jnp.int32)[:, None]
    own = parts * PT + pos[None, :]
    last_a = jnp.clip(pos - (PT - HALO_T), 0, HALO_T - 1)
    upper = (parts + 1) * PT + border[:, last_a]
    upper = jnp.where(parts == NPART - 1, own, upper)
    first_c = jnp.clip(pos, 0, HALO_T - 1)
    prev_inv = jnp.roll(border_inv, 1, axis=0)
    lower = (parts - 1) * PT + (PT - HALO_T) + prev_inv[:, first_c]
    lower = jnp.where(parts == 0, own, lower)
    mid_m = jnp.clip(pos - HALO_T, 0, middle_len - 1)
    mid_rank = jnp.broadcast_to(middle_inv[:, mid_m], (NPART, PT))
    mid_pos = jnp.take_along_axis(middle, mid_rank ^ 1, axis=1)
    centre = parts * PT + HALO_T + mid_pos
    result = jnp.where(pos[None, :] >= PT - HALO_T, upper, jnp.where(pos[None, :] < HALO_T, lower, centre))
    return result.reshape(NT).astype(jnp.int32)


def build_graph(key):
    pair_key = jax.random.fold_in(key, 1)
    value_key = jax.random.fold_in(key, 2)
    live_key = jax.random.fold_in(key, 3)
    rows = jnp.arange(NT, dtype=jnp.int32)
    all_vals = []
    all_cols = []
    all_live = []
    for slot in range(K):
        round_key = jax.random.fold_in(pair_key, slot)
        if slot % 4 == 0:
            partner = cross_partners(round_key)
        else:
            partner = intra_partners(round_key)
        low = jnp.minimum(rows, partner)

        def one_tile(row, col, lowest):
            tile_key = jax.random.fold_in(jax.random.fold_in(value_key, slot), lowest)
            values = jax.random.uniform(jax.random.fold_in(tile_key, 1), (128, 128), jnp.float32, 0.5, 1.5)
            present = jax.random.randint(jax.random.fold_in(tile_key, 2), (128, 128), 0, 2).astype(jnp.float32)
            block = values * present
            return jnp.where(row < col, block, jnp.where(row > col, block.T, block + block.T))

        def one_live(lowest):
            draw_key = jax.random.fold_in(jax.random.fold_in(live_key, slot), lowest)
            level = jax.random.randint(draw_key, (), 0, 4)
            return (level < lowest // PT % 4 + 1).astype(jnp.int32)
        all_vals.append(jax.vmap(one_tile)(rows, partner, low))
        all_cols.append(partner)
        all_live.append(jax.vmap(one_live)(low))
    return (jnp.stack(all_vals, axis=1), jnp.stack(all_cols, axis=1), jnp.stack(all_live, axis=1))


def draw_tile_vals(key, part):
    return build_graph(jax.random.fold_in(key, 7))[0].astype(jnp.bfloat16)


def draw_tile_cols(key, part):
    return build_graph(jax.random.fold_in(key, 7))[1].astype(jnp.int32)


def draw_tile_live(key, part):
    return build_graph(jax.random.fold_in(key, 7))[2].astype(jnp.int32)


def block_levels(stream_key, dims, cuts, least, high):
    gain = 1.0
    for axis_at, shards_of in cuts:
        steps = jax.random.uniform(jax.random.fold_in(jax.random.fold_in(stream_key, 6), axis_at), (shards_of,), jnp.float32, least / len(cuts), high / len(cuts))
        gain = gain * jnp.repeat(jnp.exp(steps), dims[axis_at] // shards_of).reshape((-1,) + (1,) * (len(dims) - 1 - axis_at))
    return gain


def bell_draw(key, extent, spread, most, pieces=(), kind=jnp.bfloat16):
    drawn = spread * jax.random.normal(key, extent, jnp.float32)
    if pieces:
        drawn = drawn * block_levels(key, extent, pieces, -0.22, 0.18)
    return jnp.clip(drawn, -most, most).astype(kind)


def setup_inputs(seed: int = 0) -> dict:
    key_list = jax.random.split(jax.random.key(seed), 10)
    return {
        "x_loader": bell_draw(key_list[0], (V, F), 1.0, 6.0, ((0, 256),)),
        "owner_index": draw_owner_index(jax.random.fold_in(key_list[9], 71), 0),
        "tile_vals": draw_tile_vals(jax.random.fold_in(key_list[9], 71), 0),
        "tile_cols": draw_tile_cols(jax.random.fold_in(key_list[9], 71), 0),
        "tile_live": draw_tile_live(jax.random.fold_in(key_list[9], 71), 0),
        "w_self": bell_draw(key_list[5], (F, F), F ** -0.5, 0.25),
        "w_neigh": bell_draw(key_list[6], (F, F), 0.5, 3.0),
        "bias": bell_draw(key_list[7], (F,), 0.5, 3.0, (), jnp.float32),
        "cotangent": bell_draw(key_list[8], (V, F), 1.0, 6.0, ((0, 256),)),
    }


def reference(x_loader, owner_index, tile_vals, tile_cols, tile_live, w_self, w_neigh, bias, cotangent):
    total, width = x_loader.shape
    tiles = tile_vals.shape[0]
    slots = tile_vals.shape[1]
    groups = tiles // 8
    features = jnp.zeros((total, width), jnp.bfloat16).at[owner_index].set(x_loader)
    masked = tile_vals * tile_live.astype(jnp.bfloat16)[:, :, None, None]
    degree = 1.0 + jnp.sum(masked.astype(jnp.float32), axis=(1, 3))
    blocks_all = features.reshape(tiles, 128, width)
    masked_groups = masked.reshape(groups, 8, slots, 128, 128)
    col_groups = tile_cols.reshape(groups, 8, slots)

    def forward_group(args):
        vals, cols = args
        picked = blocks_all[cols].astype(jnp.float32)
        return jnp.einsum("gkab,gkbf->gaf", vals.astype(jnp.float32), picked)

    summed = lax.map(forward_group, (masked_groups, col_groups)).reshape(total, width)
    agg = (summed / degree.reshape(total, 1)).astype(jnp.bfloat16)
    pre = jnp.dot(features, w_self, preferred_element_type=jnp.float32) + jnp.dot(agg, w_neigh, preferred_element_type=jnp.float32) + bias.astype(jnp.float32)
    layer_out = jnp.where(pre > 0, pre, jnp.expm1(jnp.minimum(pre, 0.0))).astype(jnp.bfloat16)
    slope = jnp.where(pre > 0, 1.0, jnp.exp(jnp.minimum(pre, 0.0)))
    dz = (cotangent.astype(jnp.float32) * slope).astype(jnp.bfloat16)
    grad_self = jnp.dot(features.T, dz, preferred_element_type=jnp.float32)
    grad_neigh = jnp.dot(agg.T, dz, preferred_element_type=jnp.float32)
    grad_bias = jnp.sum(dz.astype(jnp.float32), axis=0)
    scaled = (jnp.dot(dz, w_neigh.T, preferred_element_type=jnp.float32) / degree.reshape(total, 1)).astype(jnp.bfloat16)
    scaled_groups = scaled.reshape(groups, 8, 128, width)

    def backward_group(carry, args):
        vals, cols, rows = args
        terms = jnp.einsum("gkab,gaf->gkbf", vals.astype(jnp.float32), rows.astype(jnp.float32))
        carry = carry.at[cols.reshape(-1)].add(terms.reshape(-1, 128, width))
        return carry, None

    start = jnp.zeros((tiles, 128, width), jnp.float32)
    back, _ = lax.scan(backward_group, start, (masked_groups, col_groups, scaled_groups))
    grad_features = (jnp.dot(dz, w_self.T, preferred_element_type=jnp.float32) + back.reshape(total, width)).astype(jnp.bfloat16)
    return layer_out, grad_features, grad_self, grad_neigh, grad_bias
```

```python
import jax
import jax.numpy as jnp
from jax import lax
from jax.sharding import PartitionSpec as P

HALO_T = 4


def shifted(value, axis, steps):
    count = lax.axis_size(axis)
    first, last = (max(0, -steps), min(count, count - steps))
    return lax.ppermute(value, axis, [(source, source + steps) for source in range(first, last)])


def with_halo(block, sides, width):
    for axis, dim in sides:
        count = lax.axis_size(axis)
        forward = [(i, i + 1) for i in range(count - 1)]
        backward = [(target, source) for source, target in forward]
        low = lax.ppermute(
            lax.slice_in_dim(block, block.shape[dim] - width, None, axis=dim), axis, forward
        )
        high = lax.ppermute(lax.slice_in_dim(block, 0, width, axis=dim), axis, backward)
        block = jnp.concatenate([low, block, high], axis=dim)
    return block


def contract_rows(left, right):
    return lax.dot_general(
        left, right, (((0,), (0,)), ((), ())), preferred_element_type=jnp.float32
    )


def contract_cols(left, right):
    return lax.dot_general(
        left, right, (((1,), (1,)), ((), ())), preferred_element_type=jnp.float32
    )


HALVING_BITS = (2, 3, 6, 0, 4, 7, 1, 5)


def halving_sum(blocks, axes):
    count = 1
    for axis in axes:
        count *= lax.axis_size(axis)
    place = lax.axis_index(axes)
    bits = [bit for bit in HALVING_BITS if (1 << bit) < count]
    for bit in bits:
        pairs = [(i, i ^ (1 << bit)) for i in range(count)]
        upper = ((place >> bit) & 1) == 1
        kept, sent = [], []
        for block in blocks:
            half = block.shape[0] // 2
            kept.append(jnp.where(upper, block[half:], block[:half]))
            sent.append(jnp.where(upper, block[:half], block[half:]))
        got = lax.ppermute(tuple(sent), axes, pairs)
        blocks = [k + g for k, g in zip(kept, got)]
    for bit in reversed(bits):
        pairs = [(i, i ^ (1 << bit)) for i in range(count)]
        upper = ((place >> bit) & 1) == 1
        got = lax.ppermute(tuple(blocks), axes, pairs)
        blocks = [
            jnp.where(upper, jnp.concatenate([g, b]), jnp.concatenate([b, g]))
            for b, g in zip(blocks, got)
        ]
    return blocks


def pass_rim(values, offset):
    return shifted(values.astype(jnp.bfloat16), "dom", offset).astype(values.dtype)


def shards(
    x_loader, owner_index, tile_vals, tile_cols, tile_live, w_self, w_neigh, bias, cotangent
):
    rows, width = x_loader.shape
    reps = lax.axis_size("rep")
    dom_place = lax.axis_index("dom")
    part_rows = rows * reps
    part_tiles = part_rows // 128
    row_tiles = rows // 128
    rim_rows = HALO_T * 128
    dest = owner_index // part_rows
    order = jnp.argsort(dest, stable=True)
    moved, slot = (
        lax.all_to_all(x_loader[order], "dom", split_axis=0, concat_axis=0, tiled=True),
        lax.all_to_all((owner_index % rows)[order], "dom", split_axis=0, concat_axis=0, tiled=True),
    )
    features = jnp.zeros((rows, width), jnp.bfloat16).at[slot].set(moved)
    first_tile = dom_place * part_tiles - HALO_T
    local_cols = tile_cols - first_tile
    masked = tile_vals * tile_live.astype(jnp.bfloat16)[:, :, None, None]
    degree = 1.0 + jnp.sum(masked, axis=(1, 3), dtype=jnp.float32)
    whole = lax.all_gather(features, "rep", axis=0, tiled=True)
    extended = with_halo(whole, (("dom", 0),), rim_rows)
    picked = extended.reshape(-1, 128, width)[local_cols]
    summed = jnp.einsum("tkab,tkbf->taf", masked, picked, preferred_element_type=jnp.float32)
    agg = (summed / degree[:, :, None]).reshape(rows, width).astype(jnp.bfloat16)
    pre = (
        jnp.dot(features, w_self, preferred_element_type=jnp.float32)
        + jnp.dot(agg, w_neigh, preferred_element_type=jnp.float32)
        + bias
    )
    layer_out = jnp.where(pre > 0, pre, jnp.expm1(jnp.minimum(pre, 0.0))).astype(jnp.bfloat16)
    slope = jnp.where(pre > 0, 1.0, jnp.exp(jnp.minimum(pre, 0.0)))
    dz = (cotangent.astype(jnp.float32) * slope).astype(jnp.bfloat16)
    grads, bias_sum = halving_sum(
        [
            jnp.concatenate([contract_rows(features, dz), contract_rows(agg, dz)]),
            jnp.sum(dz, axis=0, dtype=jnp.float32).reshape(256, -1),
        ],
        ("dom", "rep"),
    )
    grad_self, grad_neigh = grads[:width], grads[width:]
    grad_bias = bias_sum.reshape(width)
    scaled = (contract_cols(dz, w_neigh) / degree.reshape(rows, 1)).astype(jnp.bfloat16)
    terms = jnp.einsum(
        "tkab,taf->tkbf",
        masked,
        scaled.reshape(row_tiles, 128, width),
        preferred_element_type=jnp.float32,
    )
    span_tiles = part_tiles + 2 * HALO_T
    selector = (
        local_cols.reshape(-1)[None, :] == jnp.arange(span_tiles, dtype=jnp.int32)[:, None]
    ).astype(jnp.float32)
    buffer = jnp.einsum(
        "en,nbf->ebf", selector, terms.reshape(-1, 128, width), precision=lax.Precision.HIGHEST
    )
    buffer = buffer.reshape(span_tiles * 128, width)
    lower = buffer[:rim_rows]
    upper = buffer[rim_rows + part_rows :]
    core = buffer[rim_rows : rim_rows + part_rows]
    core = core.at[:rim_rows].add(pass_rim(upper, 1))
    core = core.at[part_rows - rim_rows :].add(pass_rim(lower, -1))
    back = lax.psum_scatter(core, "rep", scatter_dimension=0, tiled=True)
    grad_features = (contract_cols(dz, w_self) + back).astype(jnp.bfloat16)
    return (layer_out, grad_features, grad_self, grad_neigh, grad_bias)


def solution(mesh):
    return jax.shard_map(
        shards,
        mesh=mesh,
        in_specs=(
            P(("dom", "rep"), None),
            P(("dom", "rep")),
            P(("dom", "rep"), None, None, None),
            P(("dom", "rep"), None),
            P(("dom", "rep"), None),
            P(),
            P(),
            P(),
            P(("dom", "rep"), None),
        ),
        out_specs=(P(("dom", "rep"), None), P(("dom", "rep"), None), P(), P(), P()),
        check_vma=False,
    )
```

```python
import jax
import jax.numpy as jnp
from jax import lax
from jax.sharding import PartitionSpec as P

HALO_T = 4


def shifted(value, axis, steps):
    count = lax.axis_size(axis)
    first, last = (max(0, -steps), min(count, count - steps))
    return lax.ppermute(value, axis, [(source, source + steps) for source in range(first, last)])


def with_halo(block, sides, width):
    for axis, dim in sides:
        count = lax.axis_size(axis)
        forward = [(i, i + 1) for i in range(count - 1)]
        backward = [(target, source) for source, target in forward]
        low = lax.ppermute(
            lax.slice_in_dim(block, block.shape[dim] - width, None, axis=dim), axis, forward
        )
        high = lax.ppermute(lax.slice_in_dim(block, 0, width, axis=dim), axis, backward)
        block = jnp.concatenate([low, block, high], axis=dim)
    return block


def contract_rows(left, right):
    return lax.dot_general(
        left, right, (((0,), (0,)), ((), ())), preferred_element_type=jnp.float32
    )


def contract_cols(left, right):
    return lax.dot_general(
        left, right, (((1,), (1,)), ((), ())), preferred_element_type=jnp.float32
    )


HALVING_BITS = (2, 3, 6, 0, 4, 7, 1, 5)


def halving_sum(block, axes):
    count = 1
    for axis in axes:
        count *= lax.axis_size(axis)
    place = lax.axis_index(axes)
    bits = [bit for bit in HALVING_BITS if (1 << bit) < count]
    for bit in bits:
        pairs = [(i, i ^ (1 << bit)) for i in range(count)]
        upper = ((place >> bit) & 1) == 1
        half = block.shape[0] // 2
        kept = jnp.where(upper, block[half:], block[:half])
        sent = jnp.where(upper, block[:half], block[half:])
        block = kept + lax.ppermute(sent, axes, pairs)
    for bit in reversed(bits):
        pairs = [(i, i ^ (1 << bit)) for i in range(count)]
        upper = ((place >> bit) & 1) == 1
        got = lax.ppermute(block, axes, pairs)
        block = jnp.where(upper, jnp.concatenate([got, block]), jnp.concatenate([block, got]))
    return block


def gather_rep(block):
    count = lax.axis_size("rep")
    place = lax.axis_index("rep")
    parts = [block] + [
        lax.ppermute(block, "rep", [(i, (i + shift) % count) for i in range(count)])
        for shift in range(1, count)
    ]
    source = (place - jnp.arange(count)) % count
    return jnp.stack(parts)[source].reshape(count * block.shape[0], *block.shape[1:])


def pass_rim(values, offset):
    return shifted(values.astype(jnp.bfloat16), "dom", offset).astype(values.dtype)


def shards(
    x_loader, owner_index, tile_vals, tile_cols, tile_live, w_self, w_neigh, bias, cotangent
):
    rows, width = x_loader.shape
    reps = lax.axis_size("rep")
    dom_place = lax.axis_index("dom")
    part_rows = rows * reps
    part_tiles = part_rows // 128
    row_tiles = rows // 128
    rim_rows = HALO_T * 128
    dest = owner_index // part_rows
    order = jnp.argsort(dest, stable=True)
    moved, slot = (
        lax.all_to_all(x_loader[order], "dom", split_axis=0, concat_axis=0, tiled=True),
        lax.all_to_all((owner_index % rows)[order], "dom", split_axis=0, concat_axis=0, tiled=True),
    )
    features = jnp.zeros((rows, width), jnp.bfloat16).at[slot].set(moved)
    first_tile = dom_place * part_tiles - HALO_T
    local_cols = tile_cols - first_tile
    masked = tile_vals * tile_live.astype(jnp.bfloat16)[:, :, None, None]
    degree = 1.0 + jnp.sum(masked, axis=(1, 3), dtype=jnp.float32)
    whole = gather_rep(features)
    extended = with_halo(whole, (("dom", 0),), rim_rows)
    picked = extended.reshape(-1, 128, width)[local_cols]
    summed = jnp.einsum("tkab,tkbf->taf", masked, picked, preferred_element_type=jnp.float32)
    agg = (summed / degree[:, :, None]).reshape(rows, width).astype(jnp.bfloat16)
    pre = (
        jnp.dot(features, w_self, preferred_element_type=jnp.float32)
        + jnp.dot(agg, w_neigh, preferred_element_type=jnp.float32)
        + bias
    )
    layer_out = jnp.where(pre > 0, pre, jnp.expm1(jnp.minimum(pre, 0.0))).astype(jnp.bfloat16)
    slope = jnp.where(pre > 0, 1.0, jnp.exp(jnp.minimum(pre, 0.0)))
    dz = (cotangent.astype(jnp.float32) * slope).astype(jnp.bfloat16)
    lanes = 2 * width * width // 256
    packed = halving_sum(
        jnp.concatenate(
            [
                jnp.concatenate([contract_rows(features, dz), contract_rows(agg, dz)]).reshape(256, lanes),
                jnp.sum(dz, axis=0, dtype=jnp.float32).reshape(256, -1),
            ],
            axis=1,
        ),
        ("dom", "rep"),
    )
    grads = packed[:, :lanes].reshape(2 * width, width)
    grad_self, grad_neigh = grads[:width], grads[width:]
    grad_bias = packed[:, lanes:].reshape(width)
    scaled = (contract_cols(dz, w_neigh) / degree.reshape(rows, 1)).astype(jnp.bfloat16)
    terms = jnp.einsum(
        "tkab,taf->tkbf",
        masked,
        scaled.reshape(row_tiles, 128, width),
        preferred_element_type=jnp.float32,
    )
    span_tiles = part_tiles + 2 * HALO_T
    selector = (
        local_cols.reshape(-1)[None, :] == jnp.arange(span_tiles, dtype=jnp.int32)[:, None]
    ).astype(jnp.float32)
    buffer = jnp.einsum(
        "en,nbf->ebf", selector, terms.reshape(-1, 128, width), precision=lax.Precision.HIGHEST
    )
    buffer = buffer.reshape(span_tiles * 128, width)
    lower = buffer[:rim_rows]
    upper = buffer[rim_rows + part_rows :]
    core = buffer[rim_rows : rim_rows + part_rows]
    core = core.at[:rim_rows].add(pass_rim(upper, 1))
    core = core.at[part_rows - rim_rows :].add(pass_rim(lower, -1))
    back = lax.psum_scatter(core, "rep", scatter_dimension=0, tiled=True)
    grad_features = (contract_cols(dz, w_self) + back).astype(jnp.bfloat16)
    return (layer_out, grad_features, grad_self, grad_neigh, grad_bias)


def solution(mesh):
    return jax.shard_map(
        shards,
        mesh=mesh,
        in_specs=(
            P(("dom", "rep"), None),
            P(("dom", "rep")),
            P(("dom", "rep"), None, None, None),
            P(("dom", "rep"), None),
            P(("dom", "rep"), None),
            P(),
            P(),
            P(),
            P(("dom", "rep"), None),
        ),
        out_specs=(P(("dom", "rep"), None), P(("dom", "rep"), None), P(), P(), P()),
        check_vma=False,
    )
```

```python
import jax
import jax.numpy as jnp
from jax import lax
from jax.sharding import PartitionSpec as P

HALO_T = 4


def shifted(value, axis, steps):
    count = lax.axis_size(axis)
    first, last = (max(0, -steps), min(count, count - steps))
    return lax.ppermute(value, axis, [(source, source + steps) for source in range(first, last)])


def with_halo(block, sides, width):
    for axis, dim in sides:
        count = lax.axis_size(axis)
        forward = [(i, i + 1) for i in range(count - 1)]
        backward = [(target, source) for source, target in forward]
        low = lax.ppermute(
            lax.slice_in_dim(block, block.shape[dim] - width, None, axis=dim), axis, forward
        )
        high = lax.ppermute(lax.slice_in_dim(block, 0, width, axis=dim), axis, backward)
        block = jnp.concatenate([low, block, high], axis=dim)
    return block


def contract_rows(left, right):
    return lax.dot_general(
        left, right, (((0,), (0,)), ((), ())), preferred_element_type=jnp.float32
    )


def contract_cols(left, right):
    return lax.dot_general(
        left, right, (((1,), (1,)), ((), ())), preferred_element_type=jnp.float32
    )


HALVING_BITS = (2, 3, 6, 0)
DOUBLING_BITS = (4, 7, 1, 5)


def halving_sum(block, axes):
    count = 1
    for axis in axes:
        count *= lax.axis_size(axis)
    place = lax.axis_index(axes)
    bits = [bit for bit in HALVING_BITS if (1 << bit) < count]
    for bit in bits:
        pairs = [(i, i ^ (1 << bit)) for i in range(count)]
        upper = ((place >> bit) & 1) == 1
        half = block.shape[0] // 2
        kept = jnp.where(upper, block[half:], block[:half])
        sent = jnp.where(upper, block[:half], block[half:])
        block = kept + lax.ppermute(sent, axes, pairs)
    for bit in DOUBLING_BITS:
        if (1 << bit) < count:
            block = block + lax.ppermute(block, axes, [(i, i ^ (1 << bit)) for i in range(count)])
    for bit in reversed(bits):
        pairs = [(i, i ^ (1 << bit)) for i in range(count)]
        upper = ((place >> bit) & 1) == 1
        got = lax.ppermute(block, axes, pairs)
        block = jnp.where(upper, jnp.concatenate([got, block]), jnp.concatenate([block, got]))
    return block


def gather_rep(block):
    count = lax.axis_size("rep")
    place = lax.axis_index("rep")
    parts = [block] + [
        lax.ppermute(block, "rep", [(i, (i + shift) % count) for i in range(count)])
        for shift in range(1, count)
    ]
    source = (place - jnp.arange(count)) % count
    return jnp.stack(parts)[source].reshape(count * block.shape[0], *block.shape[1:])


def pass_rim(values, offset):
    return shifted(values.astype(jnp.bfloat16), "dom", offset).astype(values.dtype)


def shards(
    x_loader, owner_index, tile_vals, tile_cols, tile_live, w_self, w_neigh, bias, cotangent
):
    rows, width = x_loader.shape
    reps = lax.axis_size("rep")
    dom_place = lax.axis_index("dom")
    part_rows = rows * reps
    part_tiles = part_rows // 128
    row_tiles = rows // 128
    rim_rows = HALO_T * 128
    dest = owner_index // part_rows
    order = jnp.argsort(dest, stable=True)
    doms = lax.axis_size("dom")
    per = rows // doms
    slots = (owner_index % rows)[order].reshape(doms, per)
    code = jnp.concatenate([slots // 32, slots % 32], axis=1).astype(jnp.bfloat16)
    code = jnp.pad(code, ((0, 0), (0, 128 - 2 * per)))
    sent = jnp.concatenate([x_loader[order].reshape(doms, per * width), code], axis=1)
    got = lax.all_to_all(sent, "dom", split_axis=0, concat_axis=0, tiled=True)
    moved = got[:, : per * width].reshape(rows, width)
    codes = got[:, per * width : per * width + 2 * per].astype(jnp.int32)
    slot = (codes[:, :per] * 32 + codes[:, per:]).reshape(rows)
    features = jnp.zeros((rows, width), jnp.bfloat16).at[slot].set(moved)
    first_tile = dom_place * part_tiles - HALO_T
    local_cols = tile_cols - first_tile
    masked = tile_vals * tile_live.astype(jnp.bfloat16)[:, :, None, None]
    degree = 1.0 + jnp.sum(masked, axis=(1, 3), dtype=jnp.float32)
    whole = gather_rep(features)
    extended = with_halo(whole, (("dom", 0),), rim_rows)
    picked = extended.reshape(-1, 128, width)[local_cols]
    summed = jnp.einsum("tkab,tkbf->taf", masked, picked, preferred_element_type=jnp.float32)
    agg = (summed / degree[:, :, None]).reshape(rows, width).astype(jnp.bfloat16)
    pre = (
        jnp.dot(features, w_self, preferred_element_type=jnp.float32)
        + jnp.dot(agg, w_neigh, preferred_element_type=jnp.float32)
        + bias
    )
    layer_out = jnp.where(pre > 0, pre, jnp.expm1(jnp.minimum(pre, 0.0))).astype(jnp.bfloat16)
    slope = jnp.where(pre > 0, 1.0, jnp.exp(jnp.minimum(pre, 0.0)))
    dz = (cotangent.astype(jnp.float32) * slope).astype(jnp.bfloat16)
    lanes = 2 * width * width // 256
    packed = halving_sum(
        jnp.concatenate(
            [
                jnp.concatenate([contract_rows(features, dz), contract_rows(agg, dz)]).reshape(256, lanes),
                jnp.sum(dz, axis=0, dtype=jnp.float32).reshape(256, -1),
            ],
            axis=1,
        ),
        ("dom", "rep"),
    )
    grads = packed[:, :lanes].reshape(2 * width, width)
    grad_self, grad_neigh = grads[:width], grads[width:]
    grad_bias = packed[:, lanes:].reshape(width)
    scaled = (contract_cols(dz, w_neigh) / degree.reshape(rows, 1)).astype(jnp.bfloat16)
    terms = jnp.einsum(
        "tkab,taf->tkbf",
        masked,
        scaled.reshape(row_tiles, 128, width),
        preferred_element_type=jnp.float32,
    )
    span_tiles = part_tiles + 2 * HALO_T
    selector = (
        local_cols.reshape(-1)[None, :] == jnp.arange(span_tiles, dtype=jnp.int32)[:, None]
    ).astype(jnp.float32)
    buffer = jnp.einsum(
        "en,nbf->ebf", selector, terms.reshape(-1, 128, width), precision=lax.Precision.HIGHEST
    )
    buffer = buffer.reshape(span_tiles * 128, width)
    lower = buffer[:rim_rows]
    upper = buffer[rim_rows + part_rows :]
    core = buffer[rim_rows : rim_rows + part_rows]
    core = core.at[:rim_rows].add(pass_rim(upper, 1))
    core = core.at[part_rows - rim_rows :].add(pass_rim(lower, -1))
    back = lax.psum_scatter(core, "rep", scatter_dimension=0, tiled=True)
    grad_features = (contract_cols(dz, w_self) + back).astype(jnp.bfloat16)
    return (layer_out, grad_features, grad_self, grad_neigh, grad_bias)


def solution(mesh):
    return jax.shard_map(
        shards,
        mesh=mesh,
        in_specs=(
            P(("dom", "rep"), None),
            P(("dom", "rep")),
            P(("dom", "rep"), None, None, None),
            P(("dom", "rep"), None),
            P(("dom", "rep"), None),
            P(),
            P(),
            P(),
            P(("dom", "rep"), None),
        ),
        out_specs=(P(("dom", "rep"), None), P(("dom", "rep"), None), P(), P(), P()),
        check_vma=False,
    )
```

```python
import jax
import jax.numpy as jnp
from jax import lax
from jax.sharding import PartitionSpec as P

HALO_T = 4


def shifted(value, axis, steps):
    count = lax.axis_size(axis)
    first, last = (max(0, -steps), min(count, count - steps))
    return lax.ppermute(value, axis, [(source, source + steps) for source in range(first, last)])


def with_halo(block, sides, width):
    for axis, dim in sides:
        count = lax.axis_size(axis)
        forward = [(i, i + 1) for i in range(count - 1)]
        backward = [(target, source) for source, target in forward]
        low = lax.ppermute(
            lax.slice_in_dim(block, block.shape[dim] - width, None, axis=dim), axis, forward
        )
        high = lax.ppermute(lax.slice_in_dim(block, 0, width, axis=dim), axis, backward)
        block = jnp.concatenate([low, block, high], axis=dim)
    return block


def contract_rows(left, right):
    return lax.dot_general(
        left, right, (((0,), (0,)), ((), ())), preferred_element_type=jnp.float32
    )


def contract_cols(left, right):
    return lax.dot_general(
        left, right, (((1,), (1,)), ((), ())), preferred_element_type=jnp.float32
    )


HALVING_BITS = (2, 3, 6, 0)
DOUBLING_BITS = (4, 7, 1, 5)


def halving_sum(block, axes):
    count = 1
    for axis in axes:
        count *= lax.axis_size(axis)
    place = lax.axis_index(axes)
    bits = [bit for bit in HALVING_BITS if (1 << bit) < count]
    for bit in bits:
        pairs = [(i, i ^ (1 << bit)) for i in range(count)]
        upper = ((place >> bit) & 1) == 1
        half = block.shape[0] // 2
        kept = jnp.where(upper, block[half:], block[:half])
        sent = jnp.where(upper, block[:half], block[half:])
        block = kept + lax.ppermute(sent, axes, pairs)
    for bit in DOUBLING_BITS:
        if (1 << bit) < count:
            block = block + lax.ppermute(block, axes, [(i, i ^ (1 << bit)) for i in range(count)])
    for bit in reversed(bits):
        pairs = [(i, i ^ (1 << bit)) for i in range(count)]
        upper = ((place >> bit) & 1) == 1
        got = lax.ppermute(block, axes, pairs)
        block = jnp.where(upper, jnp.concatenate([got, block]), jnp.concatenate([block, got]))
    return block


def gather_rep(block):
    count = lax.axis_size("rep")
    place = lax.axis_index("rep")
    parts = [block] + [
        lax.ppermute(block, "rep", [(i, (i + shift) % count) for i in range(count)])
        for shift in range(1, count)
    ]
    source = (place - jnp.arange(count)) % count
    return jnp.stack(parts)[source].reshape(count * block.shape[0], *block.shape[1:])


def pass_rim(values, offset):
    return shifted(values.astype(jnp.bfloat16), "dom", offset).astype(values.dtype)


def shards(
    x_loader, owner_index, tile_vals, tile_cols, tile_live, w_self, w_neigh, bias, cotangent
):
    rows, width = x_loader.shape
    reps = lax.axis_size("rep")
    dom_place = lax.axis_index("dom")
    part_rows = rows * reps
    part_tiles = part_rows // 128
    row_tiles = rows // 128
    rim_rows = HALO_T * 128
    dest = owner_index // part_rows
    order = jnp.argsort(dest, stable=True)
    doms = lax.axis_size("dom")
    per = rows // doms
    slots = (owner_index % rows)[order].reshape(doms, per)
    code = jnp.concatenate([slots // 32, slots % 32], axis=1).astype(jnp.bfloat16)
    code = jnp.pad(code, ((0, 0), (0, 128 - 2 * per)))
    sent = jnp.concatenate([x_loader[order].reshape(doms, per * width), code], axis=1)
    got = lax.all_to_all(sent, "dom", split_axis=0, concat_axis=0, tiled=True)
    moved = got[:, : per * width].reshape(rows, width)
    codes = got[:, per * width : per * width + 2 * per].astype(jnp.int32)
    slot = (codes[:, :per] * 32 + codes[:, per:]).reshape(rows)
    features = jnp.zeros((rows, width), jnp.bfloat16).at[slot].set(moved)
    first_tile = dom_place * part_tiles - HALO_T
    local_cols = tile_cols - first_tile
    masked = tile_vals * tile_live.astype(jnp.bfloat16)[:, :, None, None]
    degree = 1.0 + jnp.sum(masked, axis=(1, 3), dtype=jnp.float32)
    whole = gather_rep(features)
    extended = with_halo(whole, (("dom", 0),), rim_rows)
    span_tiles = part_tiles + 2 * HALO_T
    onehot = (local_cols[:, :, None] == jnp.arange(span_tiles, dtype=jnp.int32)).astype(jnp.bfloat16)
    merged = jnp.einsum("tke,tkab->teab", onehot, masked, preferred_element_type=jnp.float32)
    merged_hi = merged.astype(jnp.bfloat16)
    merged_lo = (merged - merged_hi.astype(jnp.float32)).astype(jnp.bfloat16)
    span = extended.reshape(span_tiles, 128, width)
    summed = jnp.einsum(
        "teab,ebf->taf", merged_hi, span, preferred_element_type=jnp.float32
    ) + jnp.einsum("teab,ebf->taf", merged_lo, span, preferred_element_type=jnp.float32)
    agg = (summed / degree[:, :, None]).reshape(rows, width).astype(jnp.bfloat16)
    pre = (
        jnp.dot(features, w_self, preferred_element_type=jnp.float32)
        + jnp.dot(agg, w_neigh, preferred_element_type=jnp.float32)
        + bias
    )
    layer_out = jnp.where(pre > 0, pre, jnp.expm1(jnp.minimum(pre, 0.0))).astype(jnp.bfloat16)
    slope = jnp.where(pre > 0, 1.0, jnp.exp(jnp.minimum(pre, 0.0)))
    dz = (cotangent.astype(jnp.float32) * slope).astype(jnp.bfloat16)
    lanes = 2 * width * width // 256
    packed = halving_sum(
        jnp.concatenate(
            [
                jnp.concatenate([contract_rows(features, dz), contract_rows(agg, dz)]).reshape(256, lanes),
                jnp.sum(dz, axis=0, dtype=jnp.float32).reshape(256, -1),
            ],
            axis=1,
        ),
        ("dom", "rep"),
    )
    grads = packed[:, :lanes].reshape(2 * width, width)
    grad_self, grad_neigh = grads[:width], grads[width:]
    grad_bias = packed[:, lanes:].reshape(width)
    scaled = (contract_cols(dz, w_neigh) / degree.reshape(rows, 1)).astype(jnp.bfloat16)
    scaled_tiles = scaled.reshape(row_tiles, 128, width)
    buffer = jnp.einsum(
        "teab,taf->ebf", merged_hi, scaled_tiles, preferred_element_type=jnp.float32
    ) + jnp.einsum("teab,taf->ebf", merged_lo, scaled_tiles, preferred_element_type=jnp.float32)
    buffer = buffer.reshape(span_tiles * 128, width)
    lower = buffer[:rim_rows]
    upper = buffer[rim_rows + part_rows :]
    core = buffer[rim_rows : rim_rows + part_rows]
    core = core.at[:rim_rows].add(pass_rim(upper, 1))
    core = core.at[part_rows - rim_rows :].add(pass_rim(lower, -1))
    back = lax.psum_scatter(core, "rep", scatter_dimension=0, tiled=True)
    grad_features = (contract_cols(dz, w_self) + back).astype(jnp.bfloat16)
    return (layer_out, grad_features, grad_self, grad_neigh, grad_bias)


def solution(mesh):
    return jax.shard_map(
        shards,
        mesh=mesh,
        in_specs=(
            P(("dom", "rep"), None),
            P(("dom", "rep")),
            P(("dom", "rep"), None, None, None),
            P(("dom", "rep"), None),
            P(("dom", "rep"), None),
            P(),
            P(),
            P(),
            P(("dom", "rep"), None),
        ),
        out_specs=(P(("dom", "rep"), None), P(("dom", "rep"), None), P(), P(), P()),
        check_vma=False,
    )
```

```python
import jax
import jax.numpy as jnp
from jax import lax
from jax.sharding import PartitionSpec as P

HALO_T = 4


def shifted(value, axis, steps):
    count = lax.axis_size(axis)
    first, last = (max(0, -steps), min(count, count - steps))
    return lax.ppermute(value, axis, [(source, source + steps) for source in range(first, last)])


def with_halo(block, sides, width):
    for axis, dim in sides:
        count = lax.axis_size(axis)
        forward = [(i, i + 1) for i in range(count - 1)]
        backward = [(target, source) for source, target in forward]
        low = lax.ppermute(
            lax.slice_in_dim(block, block.shape[dim] - width, None, axis=dim), axis, forward
        )
        high = lax.ppermute(lax.slice_in_dim(block, 0, width, axis=dim), axis, backward)
        block = jnp.concatenate([low, block, high], axis=dim)
    return block


def contract_rows(left, right):
    return lax.dot_general(
        left, right, (((0,), (0,)), ((), ())), preferred_element_type=jnp.float32
    )


def contract_cols(left, right):
    return lax.dot_general(
        left, right, (((1,), (1,)), ((), ())), preferred_element_type=jnp.float32
    )


HALVING_BITS = (2, 3, 6, 0)
DOUBLING_BITS = (4, 7, 1, 5)


def halving_sum(block, axes):
    count = 1
    for axis in axes:
        count *= lax.axis_size(axis)
    place = lax.axis_index(axes)
    bits = [bit for bit in HALVING_BITS if (1 << bit) < count]
    for bit in bits:
        pairs = [(i, i ^ (1 << bit)) for i in range(count)]
        upper = ((place >> bit) & 1) == 1
        half = block.shape[0] // 2
        kept = jnp.where(upper, block[half:], block[:half])
        sent = jnp.where(upper, block[:half], block[half:])
        block = kept + lax.ppermute(sent, axes, pairs)
    for bit in DOUBLING_BITS:
        if (1 << bit) < count:
            block = block + lax.ppermute(block, axes, [(i, i ^ (1 << bit)) for i in range(count)])
    for bit in reversed(bits):
        pairs = [(i, i ^ (1 << bit)) for i in range(count)]
        upper = ((place >> bit) & 1) == 1
        got = lax.ppermute(block, axes, pairs)
        block = jnp.where(upper, jnp.concatenate([got, block]), jnp.concatenate([block, got]))
    return block


def gather_rep(block):
    count = lax.axis_size("rep")
    place = lax.axis_index("rep")
    parts = [block] + [
        lax.ppermute(block, "rep", [(i, (i + shift) % count) for i in range(count)])
        for shift in range(1, count)
    ]
    source = (place - jnp.arange(count)) % count
    return jnp.stack(parts)[source].reshape(count * block.shape[0], *block.shape[1:])


def pass_rim(values, offset):
    return shifted(values.astype(jnp.bfloat16), "dom", offset).astype(values.dtype)


def shards(
    x_loader, owner_index, tile_vals, tile_cols, tile_live, w_self, w_neigh, bias, cotangent
):
    rows, width = x_loader.shape
    reps = lax.axis_size("rep")
    dom_place = lax.axis_index("dom")
    part_rows = rows * reps
    part_tiles = part_rows // 128
    row_tiles = rows // 128
    rim_rows = HALO_T * 128
    dest = owner_index // part_rows
    doms = lax.axis_size("dom")
    per = rows // doms
    line = jnp.arange(rows, dtype=jnp.int32)
    dest_hot = (dest[:, None] == jnp.arange(doms, dtype=jnp.int32)).astype(jnp.bfloat16)
    earlier = (line[:, None] > line[None, :]).astype(jnp.bfloat16)
    before = jnp.dot(earlier, dest_hot, preferred_element_type=jnp.float32)
    rank = jnp.sum(before * dest_hot.astype(jnp.float32), axis=1).astype(jnp.int32)
    to_sorted = ((dest * per + rank)[None, :] == line[:, None]).astype(jnp.bfloat16)
    slot_src = owner_index % rows
    code_src = jnp.stack([slot_src // 32, slot_src % 32], axis=1).astype(jnp.bfloat16)
    code = jnp.dot(to_sorted, code_src, preferred_element_type=jnp.float32)
    code = jnp.concatenate([code[:, 0].reshape(doms, per), code[:, 1].reshape(doms, per)], axis=1)
    code = jnp.pad(code.astype(jnp.bfloat16), ((0, 0), (0, 128 - 2 * per)))
    x_sorted = jnp.dot(to_sorted, x_loader, preferred_element_type=jnp.float32).astype(jnp.bfloat16)
    sent = jnp.concatenate([x_sorted.reshape(doms, per * width), code], axis=1)
    got = lax.all_to_all(sent, "dom", split_axis=0, concat_axis=0, tiled=True)
    moved = got[:, : per * width].reshape(rows, width)
    codes = got[:, per * width : per * width + 2 * per].astype(jnp.int32)
    slot = (codes[:, :per] * 32 + codes[:, per:]).reshape(rows)
    to_owner = (slot[None, :] == line[:, None]).astype(jnp.bfloat16)
    features = jnp.dot(to_owner, moved, preferred_element_type=jnp.float32).astype(jnp.bfloat16)
    first_tile = dom_place * part_tiles - HALO_T
    local_cols = tile_cols - first_tile
    masked = tile_vals * tile_live.astype(jnp.bfloat16)[:, :, None, None]
    degree = 1.0 + jnp.sum(masked, axis=(1, 3), dtype=jnp.float32)
    whole = gather_rep(features)
    extended = with_halo(whole, (("dom", 0),), rim_rows)
    span_tiles = part_tiles + 2 * HALO_T
    onehot = (local_cols[:, :, None] == jnp.arange(span_tiles, dtype=jnp.int32)).astype(jnp.bfloat16)
    merged = jnp.einsum("tke,tkab->teab", onehot, masked, preferred_element_type=jnp.float32)
    merged_hi = merged.astype(jnp.bfloat16)
    merged_lo = (merged - merged_hi.astype(jnp.float32)).astype(jnp.bfloat16)
    span = extended.reshape(span_tiles, 128, width)
    summed = jnp.einsum(
        "teab,ebf->taf", merged_hi, span, preferred_element_type=jnp.float32
    ) + jnp.einsum("teab,ebf->taf", merged_lo, span, preferred_element_type=jnp.float32)
    agg = (summed / degree[:, :, None]).reshape(rows, width).astype(jnp.bfloat16)
    pre = (
        jnp.dot(features, w_self, preferred_element_type=jnp.float32)
        + jnp.dot(agg, w_neigh, preferred_element_type=jnp.float32)
        + bias
    )
    layer_out = jnp.where(pre > 0, pre, jnp.expm1(jnp.minimum(pre, 0.0))).astype(jnp.bfloat16)
    slope = jnp.where(pre > 0, 1.0, jnp.exp(jnp.minimum(pre, 0.0)))
    dz = (cotangent.astype(jnp.float32) * slope).astype(jnp.bfloat16)
    lanes = 2 * width * width // 256
    packed = halving_sum(
        jnp.concatenate(
            [
                jnp.concatenate([contract_rows(features, dz), contract_rows(agg, dz)]).reshape(256, lanes),
                jnp.sum(dz, axis=0, dtype=jnp.float32).reshape(256, -1),
            ],
            axis=1,
        ),
        ("dom", "rep"),
    )
    grads = packed[:, :lanes].reshape(2 * width, width)
    grad_self, grad_neigh = grads[:width], grads[width:]
    grad_bias = packed[:, lanes:].reshape(width)
    scaled = (contract_cols(dz, w_neigh) / degree.reshape(rows, 1)).astype(jnp.bfloat16)
    scaled_tiles = scaled.reshape(row_tiles, 128, width)
    buffer = jnp.einsum(
        "teab,taf->ebf", merged_hi, scaled_tiles, preferred_element_type=jnp.float32
    ) + jnp.einsum("teab,taf->ebf", merged_lo, scaled_tiles, preferred_element_type=jnp.float32)
    buffer = buffer.reshape(span_tiles * 128, width)
    lower = buffer[:rim_rows]
    upper = buffer[rim_rows + part_rows :]
    core = buffer[rim_rows : rim_rows + part_rows]
    core = core.at[:rim_rows].add(pass_rim(upper, 1))
    core = core.at[part_rows - rim_rows :].add(pass_rim(lower, -1))
    back = lax.psum_scatter(core, "rep", scatter_dimension=0, tiled=True)
    grad_features = (contract_cols(dz, w_self) + back).astype(jnp.bfloat16)
    return (layer_out, grad_features, grad_self, grad_neigh, grad_bias)


def solution(mesh):
    return jax.shard_map(
        shards,
        mesh=mesh,
        in_specs=(
            P(("dom", "rep"), None),
            P(("dom", "rep")),
            P(("dom", "rep"), None, None, None),
            P(("dom", "rep"), None),
            P(("dom", "rep"), None),
            P(),
            P(),
            P(),
            P(("dom", "rep"), None),
        ),
        out_specs=(P(("dom", "rep"), None), P(("dom", "rep"), None), P(), P(), P()),
        check_vma=False,
    )
```

```python
import jax
import jax.numpy as jnp
from jax import lax
from jax.sharding import PartitionSpec as P

HALO_T = 4


def shifted(value, axis, steps):
    count = lax.axis_size(axis)
    first, last = (max(0, -steps), min(count, count - steps))
    return lax.ppermute(value, axis, [(source, source + steps) for source in range(first, last)])


def with_halo(block, sides, width):
    for axis, dim in sides:
        count = lax.axis_size(axis)
        forward = [(i, i + 1) for i in range(count - 1)]
        backward = [(target, source) for source, target in forward]
        low = lax.ppermute(
            lax.slice_in_dim(block, block.shape[dim] - width, None, axis=dim), axis, forward
        )
        high = lax.ppermute(lax.slice_in_dim(block, 0, width, axis=dim), axis, backward)
        block = jnp.concatenate([low, block, high], axis=dim)
    return block


def contract_rows(left, right):
    return lax.dot_general(
        left, right, (((0,), (0,)), ((), ())), preferred_element_type=jnp.float32
    )


def contract_cols(left, right):
    return lax.dot_general(
        left, right, (((1,), (1,)), ((), ())), preferred_element_type=jnp.float32
    )


HALVING_ORDERS = ((2, 3, 6, 0), (2, 6, 3, 0))
DOUBLING_BITS = (4, 7, 1, 5)


def by_bit(bits, pieces, axes, count):
    got = [None] * len(pieces)
    for bit in dict.fromkeys(bits):
        group = [i for i, b in enumerate(bits) if b == bit]
        sizes = [pieces[i].shape[1] for i in group]
        joined = jnp.concatenate([pieces[i] for i in group], axis=1)
        moved = lax.ppermute(joined, axes, [(i, i ^ (1 << bit)) for i in range(count)])
        offset = 0
        for i, size in zip(group, sizes):
            got[i] = moved[:, offset : offset + size]
            offset += size
    return got


def halving_sum(block, axes):
    count = 1
    for axis in axes:
        count *= lax.axis_size(axis)
    place = lax.axis_index(axes)
    split = block.shape[1] // 256 * 128
    parts = [block[:, :split], block[:, split:]]
    stages = list(zip(*HALVING_ORDERS))
    for bits in stages:
        uppers = [((place >> bit) & 1) == 1 for bit in bits]
        half = parts[0].shape[0] // 2
        kept = [jnp.where(u, p[half:], p[:half]) for p, u in zip(parts, uppers)]
        sent = [jnp.where(u, p[:half], p[half:]) for p, u in zip(parts, uppers)]
        got = by_bit(bits, sent, axes, count)
        parts = [k + g for k, g in zip(kept, got)]
    block = jnp.concatenate(parts, axis=1)
    for bit in DOUBLING_BITS:
        block = block + lax.ppermute(block, axes, [(i, i ^ (1 << bit)) for i in range(count)])
    parts = [block[:, :split], block[:, split:]]
    for bits in reversed(stages):
        uppers = [((place >> bit) & 1) == 1 for bit in bits]
        got = by_bit(bits, parts, axes, count)
        parts = [
            jnp.where(u, jnp.concatenate([g, p]), jnp.concatenate([p, g]))
            for p, g, u in zip(parts, got, uppers)
        ]
    return jnp.concatenate(parts, axis=1)


def gather_rep(block):
    count = lax.axis_size("rep")
    place = lax.axis_index("rep")
    parts = [block] + [
        lax.ppermute(block, "rep", [(i, (i + shift) % count) for i in range(count)])
        for shift in range(1, count)
    ]
    source = (place - jnp.arange(count)) % count
    return jnp.stack(parts)[source].reshape(count * block.shape[0], *block.shape[1:])


def pass_rim(values, offset):
    return shifted(values.astype(jnp.bfloat16), "dom", offset).astype(values.dtype)


def shards(
    x_loader, owner_index, tile_vals, tile_cols, tile_live, w_self, w_neigh, bias, cotangent
):
    rows, width = x_loader.shape
    reps = lax.axis_size("rep")
    dom_place = lax.axis_index("dom")
    part_rows = rows * reps
    part_tiles = part_rows // 128
    row_tiles = rows // 128
    rim_rows = HALO_T * 128
    dest = owner_index // part_rows
    doms = lax.axis_size("dom")
    per = rows // doms
    line = jnp.arange(rows, dtype=jnp.int32)
    dest_hot = (dest[:, None] == jnp.arange(doms, dtype=jnp.int32)).astype(jnp.bfloat16)
    earlier = (line[:, None] > line[None, :]).astype(jnp.bfloat16)
    before = jnp.dot(earlier, dest_hot, preferred_element_type=jnp.float32)
    rank = jnp.sum(before * dest_hot.astype(jnp.float32), axis=1).astype(jnp.int32)
    to_sorted = ((dest * per + rank)[None, :] == line[:, None]).astype(jnp.bfloat16)
    slot_src = owner_index % rows
    code_src = jnp.stack([slot_src // 32, slot_src % 32], axis=1).astype(jnp.bfloat16)
    code = jnp.dot(to_sorted, code_src, preferred_element_type=jnp.float32)
    code = jnp.concatenate([code[:, 0].reshape(doms, per), code[:, 1].reshape(doms, per)], axis=1)
    code = jnp.pad(code.astype(jnp.bfloat16), ((0, 0), (0, 128 - 2 * per)))
    x_sorted = jnp.dot(to_sorted, x_loader, preferred_element_type=jnp.float32).astype(jnp.bfloat16)
    sent = jnp.concatenate([x_sorted.reshape(doms, per * width), code], axis=1)
    got = lax.all_to_all(sent, "dom", split_axis=0, concat_axis=0, tiled=True)
    moved = got[:, : per * width].reshape(rows, width)
    codes = got[:, per * width : per * width + 2 * per].astype(jnp.int32)
    slot = (codes[:, :per] * 32 + codes[:, per:]).reshape(rows)
    to_owner = (slot[None, :] == line[:, None]).astype(jnp.bfloat16)
    features = jnp.dot(to_owner, moved, preferred_element_type=jnp.float32).astype(jnp.bfloat16)
    first_tile = dom_place * part_tiles - HALO_T
    local_cols = tile_cols - first_tile
    masked = tile_vals * tile_live.astype(jnp.bfloat16)[:, :, None, None]
    degree = 1.0 + jnp.sum(masked, axis=(1, 3), dtype=jnp.float32)
    whole = gather_rep(features)
    extended = with_halo(whole, (("dom", 0),), rim_rows)
    span_tiles = part_tiles + 2 * HALO_T
    onehot = (local_cols[:, :, None] == jnp.arange(span_tiles, dtype=jnp.int32)).astype(jnp.bfloat16)
    merged = jnp.einsum("tke,tkab->teab", onehot, masked, preferred_element_type=jnp.float32)
    merged_hi = merged.astype(jnp.bfloat16)
    merged_lo = (merged - merged_hi.astype(jnp.float32)).astype(jnp.bfloat16)
    span = extended.reshape(span_tiles, 128, width)
    summed = jnp.einsum(
        "teab,ebf->taf", merged_hi, span, preferred_element_type=jnp.float32
    ) + jnp.einsum("teab,ebf->taf", merged_lo, span, preferred_element_type=jnp.float32)
    agg = (summed / degree[:, :, None]).reshape(rows, width).astype(jnp.bfloat16)
    pre = (
        jnp.dot(features, w_self, preferred_element_type=jnp.float32)
        + jnp.dot(agg, w_neigh, preferred_element_type=jnp.float32)
        + bias
    )
    layer_out = jnp.where(pre > 0, pre, jnp.expm1(jnp.minimum(pre, 0.0))).astype(jnp.bfloat16)
    slope = jnp.where(pre > 0, 1.0, jnp.exp(jnp.minimum(pre, 0.0)))
    dz = (cotangent.astype(jnp.float32) * slope).astype(jnp.bfloat16)
    lanes = 2 * width * width // 256
    packed = halving_sum(
        jnp.concatenate(
            [
                jnp.concatenate([contract_rows(features, dz), contract_rows(agg, dz)]).reshape(256, lanes),
                jnp.sum(dz, axis=0, dtype=jnp.float32).reshape(256, -1),
            ],
            axis=1,
        ),
        ("dom", "rep"),
    )
    grads = packed[:, :lanes].reshape(2 * width, width)
    grad_self, grad_neigh = grads[:width], grads[width:]
    grad_bias = packed[:, lanes:].reshape(width)
    scaled = (contract_cols(dz, w_neigh) / degree.reshape(rows, 1)).astype(jnp.bfloat16)
    scaled_tiles = scaled.reshape(row_tiles, 128, width)
    buffer = jnp.einsum(
        "teab,taf->ebf", merged_hi, scaled_tiles, preferred_element_type=jnp.float32
    ) + jnp.einsum("teab,taf->ebf", merged_lo, scaled_tiles, preferred_element_type=jnp.float32)
    buffer = buffer.reshape(span_tiles * 128, width)
    lower = buffer[:rim_rows]
    upper = buffer[rim_rows + part_rows :]
    core = buffer[rim_rows : rim_rows + part_rows]
    core = core.at[:rim_rows].add(pass_rim(upper, 1))
    core = core.at[part_rows - rim_rows :].add(pass_rim(lower, -1))
    back = lax.psum_scatter(core, "rep", scatter_dimension=0, tiled=True)
    grad_features = (contract_cols(dz, w_self) + back).astype(jnp.bfloat16)
    return (layer_out, grad_features, grad_self, grad_neigh, grad_bias)


def solution(mesh):
    return jax.shard_map(
        shards,
        mesh=mesh,
        in_specs=(
            P(("dom", "rep"), None),
            P(("dom", "rep")),
            P(("dom", "rep"), None, None, None),
            P(("dom", "rep"), None),
            P(("dom", "rep"), None),
            P(),
            P(),
            P(),
            P(("dom", "rep"), None),
        ),
        out_specs=(P(("dom", "rep"), None), P(("dom", "rep"), None), P(), P(), P()),
        check_vma=False,
    )
```

```python
import jax
import jax.numpy as jnp
from jax import lax
from jax.sharding import PartitionSpec as P

HALO_T = 4


def shifted(value, axis, steps):
    count = lax.axis_size(axis)
    first, last = (max(0, -steps), min(count, count - steps))
    return lax.ppermute(value, axis, [(source, source + steps) for source in range(first, last)])


def with_halo(block, sides, width):
    for axis, dim in sides:
        count = lax.axis_size(axis)
        forward = [(i, i + 1) for i in range(count - 1)]
        backward = [(target, source) for source, target in forward]
        low = lax.ppermute(
            lax.slice_in_dim(block, block.shape[dim] - width, None, axis=dim), axis, forward
        )
        high = lax.ppermute(lax.slice_in_dim(block, 0, width, axis=dim), axis, backward)
        block = jnp.concatenate([low, block, high], axis=dim)
    return block


def contract_rows(left, right):
    return lax.dot_general(
        left, right, (((0,), (0,)), ((), ())), preferred_element_type=jnp.float32
    )


def contract_cols(left, right):
    return lax.dot_general(
        left, right, (((1,), (1,)), ((), ())), preferred_element_type=jnp.float32
    )


HALVING_BITS = (2, 3, 6, 0)
DOUBLING_BITS = (4, 7, 1, 5)


def halving_sum(block, axes, held, side):
    count = 1
    for axis in axes:
        count *= lax.axis_size(axis)
    place = lax.axis_index(axes)
    bits = [bit for bit in HALVING_BITS if (1 << bit) < count]
    for bit in bits:
        pairs = [(i, i ^ (1 << bit)) for i in range(count)]
        upper = ((place >> bit) & 1) == 1
        half = block.shape[0] // 2
        kept = jnp.where(upper, block[half:], block[:half])
        sent = jnp.where(upper, block[:half], block[half:])
        block = kept + lax.ppermute(sent, axes, pairs)
        if bit == bits[0]:
            block, held = lax.optimization_barrier((block, held))
            held = side(held)
    for bit in DOUBLING_BITS:
        if (1 << bit) < count:
            block = block + lax.ppermute(block, axes, [(i, i ^ (1 << bit)) for i in range(count)])
    block, held = lax.optimization_barrier((block, held))
    for bit in reversed(bits):
        pairs = [(i, i ^ (1 << bit)) for i in range(count)]
        upper = ((place >> bit) & 1) == 1
        got = lax.ppermute(block, axes, pairs)
        block = jnp.where(upper, jnp.concatenate([got, block]), jnp.concatenate([block, got]))
    return block, held


def scatter_rep(block):
    count = lax.axis_size("rep")
    place = lax.axis_index("rep")
    tiles = block.reshape(count, block.shape[0] // count, *block.shape[1:])
    total = tiles[place]
    for shift in range(1, count):
        total = total + lax.ppermute(
            tiles[(place + shift) % count], "rep", [(i, (i + shift) % count) for i in range(count)]
        )
    return total


def gather_rep(block):
    count = lax.axis_size("rep")
    place = lax.axis_index("rep")
    parts = [block] + [
        lax.ppermute(block, "rep", [(i, (i + shift) % count) for i in range(count)])
        for shift in range(1, count)
    ]
    source = (place - jnp.arange(count)) % count
    return jnp.stack(parts)[source].reshape(count * block.shape[0], *block.shape[1:])


def pass_rim(values, offset):
    return shifted(values.astype(jnp.bfloat16), "dom", offset).astype(values.dtype)


def shards(
    x_loader, owner_index, tile_vals, tile_cols, tile_live, w_self, w_neigh, bias, cotangent
):
    rows, width = x_loader.shape
    reps = lax.axis_size("rep")
    dom_place = lax.axis_index("dom")
    part_rows = rows * reps
    part_tiles = part_rows // 128
    row_tiles = rows // 128
    rim_rows = HALO_T * 128
    dest = owner_index // part_rows
    doms = lax.axis_size("dom")
    per = rows // doms
    line = jnp.arange(rows, dtype=jnp.int32)
    dest_hot = (dest[:, None] == jnp.arange(doms, dtype=jnp.int32)).astype(jnp.bfloat16)
    earlier = (line[:, None] > line[None, :]).astype(jnp.bfloat16)
    before = jnp.dot(earlier, dest_hot, preferred_element_type=jnp.float32)
    rank = jnp.sum(before * dest_hot.astype(jnp.float32), axis=1).astype(jnp.int32)
    to_sorted = ((dest * per + rank)[None, :] == line[:, None]).astype(jnp.bfloat16)
    slot_src = owner_index % rows
    code_src = jnp.stack([slot_src // 32, slot_src % 32], axis=1).astype(jnp.bfloat16)
    code = jnp.dot(to_sorted, code_src, preferred_element_type=jnp.float32)
    code = jnp.concatenate([code[:, 0].reshape(doms, per), code[:, 1].reshape(doms, per)], axis=1)
    code = jnp.pad(code.astype(jnp.bfloat16), ((0, 0), (0, 128 - 2 * per)))
    x_sorted = jnp.dot(to_sorted, x_loader, preferred_element_type=jnp.float32).astype(jnp.bfloat16)
    sent = jnp.concatenate([x_sorted.reshape(doms, per * width), code], axis=1)
    got = lax.all_to_all(sent, "dom", split_axis=0, concat_axis=0, tiled=True)
    moved = got[:, : per * width].reshape(rows, width)
    codes = got[:, per * width : per * width + 2 * per].astype(jnp.int32)
    slot = (codes[:, :per] * 32 + codes[:, per:]).reshape(rows)
    to_owner = (slot[None, :] == line[:, None]).astype(jnp.bfloat16)
    features = jnp.dot(to_owner, moved, preferred_element_type=jnp.float32).astype(jnp.bfloat16)
    first_tile = dom_place * part_tiles - HALO_T
    local_cols = tile_cols - first_tile
    masked = tile_vals * tile_live.astype(jnp.bfloat16)[:, :, None, None]
    degree = 1.0 + jnp.sum(masked, axis=(1, 3), dtype=jnp.float32)
    whole = gather_rep(features)
    extended = with_halo(whole, (("dom", 0),), rim_rows)
    span_tiles = part_tiles + 2 * HALO_T
    onehot = (local_cols[:, :, None] == jnp.arange(span_tiles, dtype=jnp.int32)).astype(jnp.bfloat16)
    merged = jnp.einsum("tke,tkab->teab", onehot, masked, preferred_element_type=jnp.float32)
    merged_hi = merged.astype(jnp.bfloat16)
    merged_lo = (merged - merged_hi.astype(jnp.float32)).astype(jnp.bfloat16)
    span = extended.reshape(span_tiles, 128, width)
    summed = jnp.einsum(
        "teab,ebf->taf", merged_hi, span, preferred_element_type=jnp.float32
    ) + jnp.einsum("teab,ebf->taf", merged_lo, span, preferred_element_type=jnp.float32)
    agg = (summed / degree[:, :, None]).reshape(rows, width).astype(jnp.bfloat16)
    pre = (
        jnp.dot(features, w_self, preferred_element_type=jnp.float32)
        + jnp.dot(agg, w_neigh, preferred_element_type=jnp.float32)
        + bias
    )
    layer_out = jnp.where(pre > 0, pre, jnp.expm1(jnp.minimum(pre, 0.0))).astype(jnp.bfloat16)
    slope = jnp.where(pre > 0, 1.0, jnp.exp(jnp.minimum(pre, 0.0)))
    dz = (cotangent.astype(jnp.float32) * slope).astype(jnp.bfloat16)
    scaled = (contract_cols(dz, w_neigh) / degree.reshape(rows, 1)).astype(jnp.bfloat16)
    scaled_tiles = scaled.reshape(row_tiles, 128, width)
    buffer = jnp.einsum(
        "teab,taf->ebf", merged_hi, scaled_tiles, preferred_element_type=jnp.float32
    ) + jnp.einsum("teab,taf->ebf", merged_lo, scaled_tiles, preferred_element_type=jnp.float32)
    buffer = buffer.reshape(span_tiles * 128, width)
    lower = buffer[:rim_rows]
    upper = buffer[rim_rows + part_rows :]
    core = buffer[rim_rows : rim_rows + part_rows]
    core = core.at[:rim_rows].add(pass_rim(upper, 1))
    core = core.at[part_rows - rim_rows :].add(pass_rim(lower, -1))
    lanes = 2 * width * width // 256
    packed, back = halving_sum(
        jnp.concatenate(
            [
                jnp.concatenate([contract_rows(features, dz), contract_rows(agg, dz)]).reshape(256, lanes),
                jnp.sum(dz, axis=0, dtype=jnp.float32).reshape(256, -1),
            ],
            axis=1,
        ),
        ("dom", "rep"),
        core,
        scatter_rep,
    )
    grads = packed[:, :lanes].reshape(2 * width, width)
    grad_self, grad_neigh = grads[:width], grads[width:]
    grad_bias = packed[:, lanes:].reshape(width)
    grad_features = (contract_cols(dz, w_self) + back).astype(jnp.bfloat16)
    return (layer_out, grad_features, grad_self, grad_neigh, grad_bias)


def solution(mesh):
    return jax.shard_map(
        shards,
        mesh=mesh,
        in_specs=(
            P(("dom", "rep"), None),
            P(("dom", "rep")),
            P(("dom", "rep"), None, None, None),
            P(("dom", "rep"), None),
            P(("dom", "rep"), None),
            P(),
            P(),
            P(),
            P(("dom", "rep"), None),
        ),
        out_specs=(P(("dom", "rep"), None), P(("dom", "rep"), None), P(), P(), P()),
        check_vma=False,
    )
```

```python
import jax
import jax.numpy as jnp
from jax import lax
from jax.sharding import PartitionSpec as P

HALO_T = 4


def shifted(value, axis, steps):
    count = lax.axis_size(axis)
    first, last = (max(0, -steps), min(count, count - steps))
    return lax.ppermute(value, axis, [(source, source + steps) for source in range(first, last)])


def with_halo(block, sides, width):
    for axis, dim in sides:
        count = lax.axis_size(axis)
        forward = [(i, i + 1) for i in range(count - 1)]
        backward = [(target, source) for source, target in forward]
        low = lax.ppermute(
            lax.slice_in_dim(block, block.shape[dim] - width, None, axis=dim), axis, forward
        )
        high = lax.ppermute(lax.slice_in_dim(block, 0, width, axis=dim), axis, backward)
        block = jnp.concatenate([low, block, high], axis=dim)
    return block


def contract_rows(left, right):
    return lax.dot_general(
        left, right, (((0,), (0,)), ((), ())), preferred_element_type=jnp.float32
    )


def contract_cols(left, right):
    return lax.dot_general(
        left, right, (((1,), (1,)), ((), ())), preferred_element_type=jnp.float32
    )


HALVING_BITS = (2, 3, 6, 0)
DOUBLING_BITS = (4, 7, 1, 5)


def halving_sum(block, axes):
    count = 1
    for axis in axes:
        count *= lax.axis_size(axis)
    place = lax.axis_index(axes)
    bits = [bit for bit in HALVING_BITS if (1 << bit) < count]
    for bit in bits:
        pairs = [(i, i ^ (1 << bit)) for i in range(count)]
        upper = ((place >> bit) & 1) == 1
        half = block.shape[0] // 2
        kept = jnp.where(upper, block[half:], block[:half])
        sent = jnp.where(upper, block[:half], block[half:])
        block = kept + lax.ppermute(sent, axes, pairs)
    for bit in DOUBLING_BITS:
        if (1 << bit) < count:
            block = block + lax.ppermute(block, axes, [(i, i ^ (1 << bit)) for i in range(count)])
    for bit in reversed(bits):
        pairs = [(i, i ^ (1 << bit)) for i in range(count)]
        upper = ((place >> bit) & 1) == 1
        got = lax.ppermute(block, axes, pairs)
        block = jnp.where(upper, jnp.concatenate([got, block]), jnp.concatenate([block, got]))
    return block


def gather_rep(block):
    count = lax.axis_size("rep")
    place = lax.axis_index("rep")
    parts = [block] + [
        lax.ppermute(block, "rep", [(i, (i + shift) % count) for i in range(count)])
        for shift in range(1, count)
    ]
    source = (place - jnp.arange(count)) % count
    return jnp.stack(parts)[source].reshape(count * block.shape[0], *block.shape[1:])


def pass_rim(values, offset):
    return shifted(values.astype(jnp.bfloat16), "dom", offset).astype(values.dtype)


def shards(
    x_loader, owner_index, tile_vals, tile_cols, tile_live, w_self, w_neigh, bias, cotangent
):
    rows, width = x_loader.shape
    reps = lax.axis_size("rep")
    dom_place = lax.axis_index("dom")
    part_rows = rows * reps
    part_tiles = part_rows // 128
    row_tiles = rows // 128
    rim_rows = HALO_T * 128
    dest = owner_index // part_rows
    doms = lax.axis_size("dom")
    per = rows // doms
    line = jnp.arange(rows, dtype=jnp.int32)
    dest_hot = (dest[:, None] == jnp.arange(doms, dtype=jnp.int32)).astype(jnp.bfloat16)
    earlier = (line[:, None] > line[None, :]).astype(jnp.bfloat16)
    before = jnp.dot(earlier, dest_hot, preferred_element_type=jnp.float32)
    rank = jnp.sum(before * dest_hot.astype(jnp.float32), axis=1).astype(jnp.int32)
    to_sorted = ((dest * per + rank)[None, :] == line[:, None]).astype(jnp.bfloat16)
    slot_src = owner_index % rows
    code_src = jnp.stack([slot_src // 32, slot_src % 32], axis=1).astype(jnp.bfloat16)
    code = jnp.dot(to_sorted, code_src, preferred_element_type=jnp.float32)
    code = jnp.concatenate([code[:, 0].reshape(doms, per), code[:, 1].reshape(doms, per)], axis=1)
    code = jnp.pad(code.astype(jnp.bfloat16), ((0, 0), (0, 128 - 2 * per)))
    x_sorted = jnp.dot(to_sorted, x_loader, preferred_element_type=jnp.float32).astype(jnp.bfloat16)
    sent = jnp.concatenate([x_sorted.reshape(doms, per * width), code], axis=1)
    got = lax.all_to_all(sent, "dom", split_axis=0, concat_axis=0, tiled=True)
    moved = got[:, : per * width].reshape(rows, width)
    codes = got[:, per * width : per * width + 2 * per].astype(jnp.int32)
    slot = (codes[:, :per] * 32 + codes[:, per:]).reshape(rows)
    to_owner = (slot[None, :] == line[:, None]).astype(jnp.bfloat16)
    features = jnp.dot(to_owner, moved, preferred_element_type=jnp.float32).astype(jnp.bfloat16)
    first_tile = dom_place * part_tiles - HALO_T
    local_cols = tile_cols - first_tile
    masked = tile_vals * tile_live.astype(jnp.bfloat16)[:, :, None, None]
    degree = 1.0 + jnp.sum(masked, axis=(1, 3), dtype=jnp.float32)
    whole = gather_rep(features)
    extended = with_halo(whole, (("dom", 0),), rim_rows)
    span_tiles = part_tiles + 2 * HALO_T
    onehot = (local_cols[:, :, None] == jnp.arange(span_tiles, dtype=jnp.int32)).astype(jnp.bfloat16)
    merged = jnp.einsum("tke,tkab->teab", onehot, masked, preferred_element_type=jnp.float32)
    merged_hi = merged.astype(jnp.bfloat16)
    merged_lo = (merged - merged_hi.astype(jnp.float32)).astype(jnp.bfloat16)
    span = extended.reshape(span_tiles, 128, width)
    summed = jnp.einsum(
        "teab,ebf->taf", merged_hi, span, preferred_element_type=jnp.float32
    ) + jnp.einsum("teab,ebf->taf", merged_lo, span, preferred_element_type=jnp.float32)
    agg = (summed / degree[:, :, None]).reshape(rows, width).astype(jnp.bfloat16)
    pre = (
        jnp.dot(features, w_self, preferred_element_type=jnp.float32)
        + jnp.dot(agg, w_neigh, preferred_element_type=jnp.float32)
        + bias
    )
    layer_out = jnp.where(pre > 0, pre, jnp.expm1(jnp.minimum(pre, 0.0))).astype(jnp.bfloat16)
    slope = jnp.where(pre > 0, 1.0, jnp.exp(jnp.minimum(pre, 0.0)))
    dz = (cotangent.astype(jnp.float32) * slope).astype(jnp.bfloat16)
    lanes = 2 * width * width // 256
    packed = halving_sum(
        jnp.concatenate(
            [
                jnp.concatenate([contract_rows(features, dz), contract_rows(agg, dz)]).reshape(256, lanes),
                jnp.pad(jnp.sum(dz, axis=0, dtype=jnp.float32).reshape(256, -1), ((0, 0), (0, 126))),
            ],
            axis=1,
        ),
        ("dom", "rep"),
    )
    grads = packed[:, :lanes].reshape(2 * width, width)
    grad_self, grad_neigh = grads[:width], grads[width:]
    grad_bias = packed[:, lanes : lanes + 2].reshape(width)
    scaled = (contract_cols(dz, w_neigh) / degree.reshape(rows, 1)).astype(jnp.bfloat16)
    scaled_tiles = scaled.reshape(row_tiles, 128, width)
    buffer = jnp.einsum(
        "teab,taf->ebf", merged_hi, scaled_tiles, preferred_element_type=jnp.float32
    ) + jnp.einsum("teab,taf->ebf", merged_lo, scaled_tiles, preferred_element_type=jnp.float32)
    buffer = buffer.reshape(span_tiles * 128, width)
    lower = buffer[:rim_rows]
    upper = buffer[rim_rows + part_rows :]
    core = buffer[rim_rows : rim_rows + part_rows]
    core = core.at[:rim_rows].add(pass_rim(upper, 1))
    core = core.at[part_rows - rim_rows :].add(pass_rim(lower, -1))
    back = lax.psum_scatter(core, "rep", scatter_dimension=0, tiled=True)
    grad_features = (contract_cols(dz, w_self) + back).astype(jnp.bfloat16)
    return (layer_out, grad_features, grad_self, grad_neigh, grad_bias)


def solution(mesh):
    return jax.shard_map(
        shards,
        mesh=mesh,
        in_specs=(
            P(("dom", "rep"), None),
            P(("dom", "rep")),
            P(("dom", "rep"), None, None, None),
            P(("dom", "rep"), None),
            P(("dom", "rep"), None),
            P(),
            P(),
            P(),
            P(("dom", "rep"), None),
        ),
        out_specs=(P(("dom", "rep"), None), P(("dom", "rep"), None), P(), P(), P()),
        check_vma=False,
    )
```

```python
import jax
import jax.numpy as jnp
from jax import lax
from jax.sharding import PartitionSpec as P

HALO_T = 4


def shifted(value, axis, steps):
    count = lax.axis_size(axis)
    first, last = (max(0, -steps), min(count, count - steps))
    return lax.ppermute(value, axis, [(source, source + steps) for source in range(first, last)])


def with_halo(block, sides, width):
    for axis, dim in sides:
        count = lax.axis_size(axis)
        forward = [(i, i + 1) for i in range(count - 1)]
        backward = [(target, source) for source, target in forward]
        low = lax.ppermute(
            lax.slice_in_dim(block, block.shape[dim] - width, None, axis=dim), axis, forward
        )
        high = lax.ppermute(lax.slice_in_dim(block, 0, width, axis=dim), axis, backward)
        block = jnp.concatenate([low, block, high], axis=dim)
    return block


def contract_rows(left, right):
    return lax.dot_general(
        left, right, (((0,), (0,)), ((), ())), preferred_element_type=jnp.float32
    )


def contract_cols(left, right):
    return lax.dot_general(
        left, right, (((1,), (1,)), ((), ())), preferred_element_type=jnp.float32
    )


HALVING_BITS = (2, 3, 6, 0)
DOUBLING_BITS = (4, 7, 1, 5)


def halving_sum(block, axes, held, side, at=1):
    count = 1
    for axis in axes:
        count *= lax.axis_size(axis)
    place = lax.axis_index(axes)
    bits = [bit for bit in HALVING_BITS if (1 << bit) < count]
    for bit in bits:
        pairs = [(i, i ^ (1 << bit)) for i in range(count)]
        upper = ((place >> bit) & 1) == 1
        half = block.shape[0] // 2
        kept = jnp.where(upper, block[half:], block[:half])
        sent = jnp.where(upper, block[:half], block[half:])
        if bit == bits[at]:
            sent, held = lax.optimization_barrier((sent, held))
            got = lax.ppermute(sent, axes, pairs)
            held = side(held)
            got, held = lax.optimization_barrier((got, held))
            block = kept + got
        else:
            block = kept + lax.ppermute(sent, axes, pairs)
    for bit in DOUBLING_BITS:
        if (1 << bit) < count:
            block = block + lax.ppermute(block, axes, [(i, i ^ (1 << bit)) for i in range(count)])
    for bit in reversed(bits):
        pairs = [(i, i ^ (1 << bit)) for i in range(count)]
        upper = ((place >> bit) & 1) == 1
        got = lax.ppermute(block, axes, pairs)
        block = jnp.where(upper, jnp.concatenate([got, block]), jnp.concatenate([block, got]))
    return block, held


def gather_rep(block):
    count = lax.axis_size("rep")
    place = lax.axis_index("rep")
    parts = [block] + [
        lax.ppermute(block, "rep", [(i, (i + shift) % count) for i in range(count)])
        for shift in range(1, count)
    ]
    source = (place - jnp.arange(count)) % count
    return jnp.stack(parts)[source].reshape(count * block.shape[0], *block.shape[1:])


def pass_rim(values, offset):
    return shifted(values.astype(jnp.bfloat16), "dom", offset).astype(values.dtype)


def shards(
    x_loader, owner_index, tile_vals, tile_cols, tile_live, w_self, w_neigh, bias, cotangent
):
    rows, width = x_loader.shape
    reps = lax.axis_size("rep")
    dom_place = lax.axis_index("dom")
    part_rows = rows * reps
    part_tiles = part_rows // 128
    row_tiles = rows // 128
    rim_rows = HALO_T * 128
    dest = owner_index // part_rows
    doms = lax.axis_size("dom")
    per = rows // doms
    line = jnp.arange(rows, dtype=jnp.int32)
    dest_hot = (dest[:, None] == jnp.arange(doms, dtype=jnp.int32)).astype(jnp.bfloat16)
    earlier = (line[:, None] > line[None, :]).astype(jnp.bfloat16)
    before = jnp.dot(earlier, dest_hot, preferred_element_type=jnp.float32)
    rank = jnp.sum(before * dest_hot.astype(jnp.float32), axis=1).astype(jnp.int32)
    to_sorted = ((dest * per + rank)[None, :] == line[:, None]).astype(jnp.bfloat16)
    slot_src = owner_index % rows
    code_src = jnp.stack([slot_src // 32, slot_src % 32], axis=1).astype(jnp.bfloat16)
    code = jnp.dot(to_sorted, code_src, preferred_element_type=jnp.float32)
    code = jnp.concatenate([code[:, 0].reshape(doms, per), code[:, 1].reshape(doms, per)], axis=1)
    code = jnp.pad(code.astype(jnp.bfloat16), ((0, 0), (0, 128 - 2 * per)))
    x_sorted = jnp.dot(to_sorted, x_loader, preferred_element_type=jnp.float32).astype(jnp.bfloat16)
    sent = jnp.concatenate([x_sorted.reshape(doms, per * width), code], axis=1)
    got = lax.all_to_all(sent, "dom", split_axis=0, concat_axis=0, tiled=True)
    moved = got[:, : per * width].reshape(rows, width)
    codes = got[:, per * width : per * width + 2 * per].astype(jnp.int32)
    slot = (codes[:, :per] * 32 + codes[:, per:]).reshape(rows)
    to_owner = (slot[None, :] == line[:, None]).astype(jnp.bfloat16)
    features = jnp.dot(to_owner, moved, preferred_element_type=jnp.float32).astype(jnp.bfloat16)
    first_tile = dom_place * part_tiles - HALO_T
    local_cols = tile_cols - first_tile
    masked = tile_vals * tile_live.astype(jnp.bfloat16)[:, :, None, None]
    degree = 1.0 + jnp.sum(masked, axis=(1, 3), dtype=jnp.float32)
    whole = gather_rep(features)
    extended = with_halo(whole, (("dom", 0),), rim_rows)
    span_tiles = part_tiles + 2 * HALO_T
    onehot = (local_cols[:, :, None] == jnp.arange(span_tiles, dtype=jnp.int32)).astype(jnp.bfloat16)
    merged = jnp.einsum("tke,tkab->teab", onehot, masked, preferred_element_type=jnp.float32)
    merged_hi = merged.astype(jnp.bfloat16)
    merged_lo = (merged - merged_hi.astype(jnp.float32)).astype(jnp.bfloat16)
    span = extended.reshape(span_tiles, 128, width)
    summed = jnp.einsum(
        "teab,ebf->taf", merged_hi, span, preferred_element_type=jnp.float32
    ) + jnp.einsum("teab,ebf->taf", merged_lo, span, preferred_element_type=jnp.float32)
    agg = (summed / degree[:, :, None]).reshape(rows, width).astype(jnp.bfloat16)
    pre = (
        jnp.dot(features, w_self, preferred_element_type=jnp.float32)
        + jnp.dot(agg, w_neigh, preferred_element_type=jnp.float32)
        + bias
    )
    layer_out = jnp.where(pre > 0, pre, jnp.expm1(jnp.minimum(pre, 0.0))).astype(jnp.bfloat16)
    slope = jnp.where(pre > 0, 1.0, jnp.exp(jnp.minimum(pre, 0.0)))
    dz = (cotangent.astype(jnp.float32) * slope).astype(jnp.bfloat16)
    def backward(dz):
        scaled = (contract_cols(dz, w_neigh) / degree.reshape(rows, 1)).astype(jnp.bfloat16)
        scaled_tiles = scaled.reshape(row_tiles, 128, width)
        buffer = jnp.einsum(
            "teab,taf->ebf", merged_hi, scaled_tiles, preferred_element_type=jnp.float32
        ) + jnp.einsum("teab,taf->ebf", merged_lo, scaled_tiles, preferred_element_type=jnp.float32)
        buffer = buffer.reshape(span_tiles * 128, width)
        lower = buffer[:rim_rows]
        upper = buffer[rim_rows + part_rows :]
        core = buffer[rim_rows : rim_rows + part_rows]
        core = core.at[:rim_rows].add(pass_rim(upper, 1))
        core = core.at[part_rows - rim_rows :].add(pass_rim(lower, -1))
        return core

    lanes = 2 * width * width // 256
    packed, core = halving_sum(
        jnp.concatenate(
            [
                jnp.concatenate([contract_rows(features, dz), contract_rows(agg, dz)]).reshape(256, lanes),
                jnp.pad(jnp.sum(dz, axis=0, dtype=jnp.float32).reshape(256, -1), ((0, 0), (0, 126))),
            ],
            axis=1,
        ),
        ("dom", "rep"),
        dz,
        backward,
    )
    grads = packed[:, :lanes].reshape(2 * width, width)
    grad_self, grad_neigh = grads[:width], grads[width:]
    grad_bias = packed[:, lanes : lanes + 2].reshape(width)
    back = lax.psum_scatter(core, "rep", scatter_dimension=0, tiled=True)
    grad_features = (contract_cols(dz, w_self) + back).astype(jnp.bfloat16)
    return (layer_out, grad_features, grad_self, grad_neigh, grad_bias)


def solution(mesh):
    return jax.shard_map(
        shards,
        mesh=mesh,
        in_specs=(
            P(("dom", "rep"), None),
            P(("dom", "rep")),
            P(("dom", "rep"), None, None, None),
            P(("dom", "rep"), None),
            P(("dom", "rep"), None),
            P(),
            P(),
            P(),
            P(("dom", "rep"), None),
        ),
        out_specs=(P(("dom", "rep"), None), P(("dom", "rep"), None), P(), P(), P()),
        check_vma=False,
    )
```

```python
import jax
import jax.numpy as jnp
from jax import lax
from jax.sharding import PartitionSpec as P

HALO_T = 4


def shifted(value, axis, steps):
    count = lax.axis_size(axis)
    first, last = (max(0, -steps), min(count, count - steps))
    return lax.ppermute(value, axis, [(source, source + steps) for source in range(first, last)])


def with_halo(block, sides, width):
    for axis, dim in sides:
        count = lax.axis_size(axis)
        forward = [(i, i + 1) for i in range(count - 1)]
        backward = [(target, source) for source, target in forward]
        low = lax.ppermute(
            lax.slice_in_dim(block, block.shape[dim] - width, None, axis=dim), axis, forward
        )
        high = lax.ppermute(lax.slice_in_dim(block, 0, width, axis=dim), axis, backward)
        block = jnp.concatenate([low, block, high], axis=dim)
    return block


def contract_rows(left, right):
    return lax.dot_general(
        left, right, (((0,), (0,)), ((), ())), preferred_element_type=jnp.float32
    )


def contract_cols(left, right):
    return lax.dot_general(
        left, right, (((1,), (1,)), ((), ())), preferred_element_type=jnp.float32
    )


HALVING_BITS = (2, 3, 6, 0)
DOUBLING_BITS = (4, 7, 5, 1)


def halving_sum(block, axes):
    count = 1
    for axis in axes:
        count *= lax.axis_size(axis)
    place = lax.axis_index(axes)
    bits = [bit for bit in HALVING_BITS if (1 << bit) < count]
    for bit in bits:
        pairs = [(i, i ^ (1 << bit)) for i in range(count)]
        upper = ((place >> bit) & 1) == 1
        half = block.shape[0] // 2
        kept = jnp.where(upper, block[half:], block[:half])
        sent = jnp.where(upper, block[:half], block[half:])
        block = kept + lax.ppermute(sent, axes, pairs)
    for bit in DOUBLING_BITS:
        if (1 << bit) < count:
            block = block + lax.ppermute(block, axes, [(i, i ^ (1 << bit)) for i in range(count)])
    for bit in reversed(bits):
        pairs = [(i, i ^ (1 << bit)) for i in range(count)]
        upper = ((place >> bit) & 1) == 1
        got = lax.ppermute(block, axes, pairs)
        block = jnp.where(upper, jnp.concatenate([got, block]), jnp.concatenate([block, got]))
    return block


def gather_rep(block):
    count = lax.axis_size("rep")
    place = lax.axis_index("rep")
    parts = [block] + [
        lax.ppermute(block, "rep", [(i, (i + shift) % count) for i in range(count)])
        for shift in range(1, count)
    ]
    source = (place - jnp.arange(count)) % count
    return jnp.stack(parts)[source].reshape(count * block.shape[0], *block.shape[1:])


def pass_rim(values, offset):
    return shifted(values.astype(jnp.bfloat16), "dom", offset).astype(values.dtype)


def shards(
    x_loader, owner_index, tile_vals, tile_cols, tile_live, w_self, w_neigh, bias, cotangent
):
    rows, width = x_loader.shape
    reps = lax.axis_size("rep")
    dom_place = lax.axis_index("dom")
    part_rows = rows * reps
    part_tiles = part_rows // 128
    row_tiles = rows // 128
    rim_rows = HALO_T * 128
    dest = owner_index // part_rows
    doms = lax.axis_size("dom")
    per = rows // doms
    line = jnp.arange(rows, dtype=jnp.int32)
    dest_hot = (dest[:, None] == jnp.arange(doms, dtype=jnp.int32)).astype(jnp.bfloat16)
    earlier = (line[:, None] > line[None, :]).astype(jnp.bfloat16)
    before = jnp.dot(earlier, dest_hot, preferred_element_type=jnp.float32)
    rank = jnp.sum(before * dest_hot.astype(jnp.float32), axis=1).astype(jnp.int32)
    to_sorted = ((dest * per + rank)[None, :] == line[:, None]).astype(jnp.bfloat16)
    slot_src = owner_index % rows
    code_src = jnp.stack([slot_src // 32, slot_src % 32], axis=1).astype(jnp.bfloat16)
    code = jnp.dot(to_sorted, code_src, preferred_element_type=jnp.float32)
    code = jnp.concatenate([code[:, 0].reshape(doms, per), code[:, 1].reshape(doms, per)], axis=1)
    code = jnp.pad(code.astype(jnp.bfloat16), ((0, 0), (0, 128 - 2 * per)))
    x_sorted = jnp.dot(to_sorted, x_loader, preferred_element_type=jnp.float32).astype(jnp.bfloat16)
    sent = jnp.concatenate([x_sorted.reshape(doms, per * width), code], axis=1)
    got = lax.all_to_all(sent, "dom", split_axis=0, concat_axis=0, tiled=True)
    moved = got[:, : per * width].reshape(rows, width)
    codes = got[:, per * width : per * width + 2 * per].astype(jnp.int32)
    slot = (codes[:, :per] * 32 + codes[:, per:]).reshape(rows)
    to_owner = (slot[None, :] == line[:, None]).astype(jnp.bfloat16)
    features = jnp.dot(to_owner, moved, preferred_element_type=jnp.float32).astype(jnp.bfloat16)
    first_tile = dom_place * part_tiles - HALO_T
    local_cols = tile_cols - first_tile
    masked = tile_vals * tile_live.astype(jnp.bfloat16)[:, :, None, None]
    degree = 1.0 + jnp.sum(masked, axis=(1, 3), dtype=jnp.float32)
    whole = gather_rep(features)
    extended = with_halo(whole, (("dom", 0),), rim_rows)
    span_tiles = part_tiles + 2 * HALO_T
    onehot = (local_cols[:, :, None] == jnp.arange(span_tiles, dtype=jnp.int32)).astype(jnp.bfloat16)
    merged = jnp.einsum("tke,tkab->teab", onehot, masked, preferred_element_type=jnp.float32)
    merged_hi = merged.astype(jnp.bfloat16)
    merged_lo = (merged - merged_hi.astype(jnp.float32)).astype(jnp.bfloat16)
    span = extended.reshape(span_tiles, 128, width)
    summed = jnp.einsum(
        "teab,ebf->taf", merged_hi, span, preferred_element_type=jnp.float32
    ) + jnp.einsum("teab,ebf->taf", merged_lo, span, preferred_element_type=jnp.float32)
    agg = (summed / degree[:, :, None]).reshape(rows, width).astype(jnp.bfloat16)
    pre = (
        jnp.dot(features, w_self, preferred_element_type=jnp.float32)
        + jnp.dot(agg, w_neigh, preferred_element_type=jnp.float32)
        + bias
    )
    layer_out = jnp.where(pre > 0, pre, jnp.expm1(jnp.minimum(pre, 0.0))).astype(jnp.bfloat16)
    slope = jnp.where(pre > 0, 1.0, jnp.exp(jnp.minimum(pre, 0.0)))
    dz = (cotangent.astype(jnp.float32) * slope).astype(jnp.bfloat16)
    lanes = 2 * width * width // 256
    packed = halving_sum(
        jnp.concatenate(
            [
                jnp.concatenate([contract_rows(features, dz), contract_rows(agg, dz)]).reshape(256, lanes),
                jnp.pad(jnp.sum(dz, axis=0, dtype=jnp.float32).reshape(256, -1), ((0, 0), (0, 126))),
            ],
            axis=1,
        ),
        ("dom", "rep"),
    )
    grads = packed[:, :lanes].reshape(2 * width, width)
    grad_self, grad_neigh = grads[:width], grads[width:]
    grad_bias = packed[:, lanes : lanes + 2].reshape(width)
    scaled = (contract_cols(dz, w_neigh) / degree.reshape(rows, 1)).astype(jnp.bfloat16)
    scaled_tiles = scaled.reshape(row_tiles, 128, width)
    buffer = jnp.einsum(
        "teab,taf->ebf", merged_hi, scaled_tiles, preferred_element_type=jnp.float32
    ) + jnp.einsum("teab,taf->ebf", merged_lo, scaled_tiles, preferred_element_type=jnp.float32)
    buffer = buffer.reshape(span_tiles * 128, width)
    lower = buffer[:rim_rows]
    upper = buffer[rim_rows + part_rows :]
    core = buffer[rim_rows : rim_rows + part_rows]
    core = core.at[:rim_rows].add(pass_rim(upper, 1))
    core = core.at[part_rows - rim_rows :].add(pass_rim(lower, -1))
    back = lax.psum_scatter(core, "rep", scatter_dimension=0, tiled=True)
    grad_features = (contract_cols(dz, w_self) + back).astype(jnp.bfloat16)
    return (layer_out, grad_features, grad_self, grad_neigh, grad_bias)


def solution(mesh):
    return jax.shard_map(
        shards,
        mesh=mesh,
        in_specs=(
            P(("dom", "rep"), None),
            P(("dom", "rep")),
            P(("dom", "rep"), None, None, None),
            P(("dom", "rep"), None),
            P(("dom", "rep"), None),
            P(),
            P(),
            P(),
            P(("dom", "rep"), None),
        ),
        out_specs=(P(("dom", "rep"), None), P(("dom", "rep"), None), P(), P(), P()),
        check_vma=False,
    )
```

```python
import jax
import jax.numpy as jnp
from jax import lax
from jax.sharding import PartitionSpec as P

HALO_T = 4


def shifted(value, axis, steps):
    count = lax.axis_size(axis)
    first, last = (max(0, -steps), min(count, count - steps))
    return lax.ppermute(value, axis, [(source, source + steps) for source in range(first, last)])


def with_halo(block, sides, width):
    for axis, dim in sides:
        count = lax.axis_size(axis)
        forward = [(i, i + 1) for i in range(count - 1)]
        backward = [(target, source) for source, target in forward]
        low = lax.ppermute(
            lax.slice_in_dim(block, block.shape[dim] - width, None, axis=dim), axis, forward
        )
        high = lax.ppermute(lax.slice_in_dim(block, 0, width, axis=dim), axis, backward)
        block = jnp.concatenate([low, block, high], axis=dim)
    return block


def contract_rows(left, right):
    return lax.dot_general(
        left, right, (((0,), (0,)), ((), ())), preferred_element_type=jnp.float32
    )


def contract_cols(left, right):
    return lax.dot_general(
        left, right, (((1,), (1,)), ((), ())), preferred_element_type=jnp.float32
    )


HALVING_BITS = (2, 6, 3, 0)
DOUBLING_BITS = (4, 7, 5, 1)


def halving_sum(block, axes):
    count = 1
    for axis in axes:
        count *= lax.axis_size(axis)
    place = lax.axis_index(axes)
    bits = [bit for bit in HALVING_BITS if (1 << bit) < count]
    for bit in bits:
        pairs = [(i, i ^ (1 << bit)) for i in range(count)]
        upper = ((place >> bit) & 1) == 1
        half = block.shape[0] // 2
        kept = jnp.where(upper, block[half:], block[:half])
        sent = jnp.where(upper, block[:half], block[half:])
        block = kept + lax.ppermute(sent, axes, pairs)
    for bit in DOUBLING_BITS:
        if (1 << bit) < count:
            block = block + lax.ppermute(block, axes, [(i, i ^ (1 << bit)) for i in range(count)])
    for bit in reversed(bits):
        pairs = [(i, i ^ (1 << bit)) for i in range(count)]
        upper = ((place >> bit) & 1) == 1
        got = lax.ppermute(block, axes, pairs)
        block = jnp.where(upper, jnp.concatenate([got, block]), jnp.concatenate([block, got]))
    return block


def gather_rep(block):
    count = lax.axis_size("rep")
    place = lax.axis_index("rep")
    parts = [block] + [
        lax.ppermute(block, "rep", [(i, (i + shift) % count) for i in range(count)])
        for shift in range(1, count)
    ]
    source = (place - jnp.arange(count)) % count
    return jnp.stack(parts)[source].reshape(count * block.shape[0], *block.shape[1:])


def pass_rim(values, offset):
    return shifted(values.astype(jnp.bfloat16), "dom", offset).astype(values.dtype)


def shards(
    x_loader, owner_index, tile_vals, tile_cols, tile_live, w_self, w_neigh, bias, cotangent
):
    rows, width = x_loader.shape
    reps = lax.axis_size("rep")
    dom_place = lax.axis_index("dom")
    part_rows = rows * reps
    part_tiles = part_rows // 128
    row_tiles = rows // 128
    rim_rows = HALO_T * 128
    dest = owner_index // part_rows
    doms = lax.axis_size("dom")
    per = rows // doms
    line = jnp.arange(rows, dtype=jnp.int32)
    dest_hot = (dest[:, None] == jnp.arange(doms, dtype=jnp.int32)).astype(jnp.bfloat16)
    earlier = (line[:, None] > line[None, :]).astype(jnp.bfloat16)
    before = jnp.dot(earlier, dest_hot, preferred_element_type=jnp.float32)
    rank = jnp.sum(before * dest_hot.astype(jnp.float32), axis=1).astype(jnp.int32)
    to_sorted = ((dest * per + rank)[None, :] == line[:, None]).astype(jnp.bfloat16)
    slot_src = owner_index % rows
    code_src = jnp.stack([slot_src // 32, slot_src % 32], axis=1).astype(jnp.bfloat16)
    code = jnp.dot(to_sorted, code_src, preferred_element_type=jnp.float32)
    code = jnp.concatenate([code[:, 0].reshape(doms, per), code[:, 1].reshape(doms, per)], axis=1)
    code = jnp.pad(code.astype(jnp.bfloat16), ((0, 0), (0, 128 - 2 * per)))
    x_sorted = jnp.dot(to_sorted, x_loader, preferred_element_type=jnp.float32).astype(jnp.bfloat16)
    sent = jnp.concatenate([x_sorted.reshape(doms, per * width), code], axis=1)
    got = lax.all_to_all(sent, "dom", split_axis=0, concat_axis=0, tiled=True)
    moved = got[:, : per * width].reshape(rows, width)
    codes = got[:, per * width : per * width + 2 * per].astype(jnp.int32)
    slot = (codes[:, :per] * 32 + codes[:, per:]).reshape(rows)
    to_owner = (slot[None, :] == line[:, None]).astype(jnp.bfloat16)
    features = jnp.dot(to_owner, moved, preferred_element_type=jnp.float32).astype(jnp.bfloat16)
    first_tile = dom_place * part_tiles - HALO_T
    local_cols = tile_cols - first_tile
    masked = tile_vals * tile_live.astype(jnp.bfloat16)[:, :, None, None]
    degree = 1.0 + jnp.sum(masked, axis=(1, 3), dtype=jnp.float32)
    whole = gather_rep(features)
    extended = with_halo(whole, (("dom", 0),), rim_rows)
    span_tiles = part_tiles + 2 * HALO_T
    onehot = (local_cols[:, :, None] == jnp.arange(span_tiles, dtype=jnp.int32)).astype(jnp.bfloat16)
    merged = jnp.einsum("tke,tkab->teab", onehot, masked, preferred_element_type=jnp.float32)
    merged_hi = merged.astype(jnp.bfloat16)
    merged_lo = (merged - merged_hi.astype(jnp.float32)).astype(jnp.bfloat16)
    span = extended.reshape(span_tiles, 128, width)
    summed = jnp.einsum(
        "teab,ebf->taf", merged_hi, span, preferred_element_type=jnp.float32
    ) + jnp.einsum("teab,ebf->taf", merged_lo, span, preferred_element_type=jnp.float32)
    agg = (summed / degree[:, :, None]).reshape(rows, width).astype(jnp.bfloat16)
    pre = (
        jnp.dot(features, w_self, preferred_element_type=jnp.float32)
        + jnp.dot(agg, w_neigh, preferred_element_type=jnp.float32)
        + bias
    )
    layer_out = jnp.where(pre > 0, pre, jnp.expm1(jnp.minimum(pre, 0.0))).astype(jnp.bfloat16)
    slope = jnp.where(pre > 0, 1.0, jnp.exp(jnp.minimum(pre, 0.0)))
    dz = (cotangent.astype(jnp.float32) * slope).astype(jnp.bfloat16)
    lanes = 2 * width * width // 256
    packed = halving_sum(
        jnp.concatenate(
            [
                jnp.concatenate([contract_rows(features, dz), contract_rows(agg, dz)]).reshape(256, lanes),
                jnp.pad(jnp.sum(dz, axis=0, dtype=jnp.float32).reshape(256, -1), ((0, 0), (0, 126))),
            ],
            axis=1,
        ),
        ("dom", "rep"),
    )
    grads = packed[:, :lanes].reshape(2 * width, width)
    grad_self, grad_neigh = grads[:width], grads[width:]
    grad_bias = packed[:, lanes : lanes + 2].reshape(width)
    scaled = (contract_cols(dz, w_neigh) / degree.reshape(rows, 1)).astype(jnp.bfloat16)
    scaled_tiles = scaled.reshape(row_tiles, 128, width)
    buffer = jnp.einsum(
        "teab,taf->ebf", merged_hi, scaled_tiles, preferred_element_type=jnp.float32
    ) + jnp.einsum("teab,taf->ebf", merged_lo, scaled_tiles, preferred_element_type=jnp.float32)
    buffer = buffer.reshape(span_tiles * 128, width)
    lower = buffer[:rim_rows]
    upper = buffer[rim_rows + part_rows :]
    core = buffer[rim_rows : rim_rows + part_rows]
    core = core.at[:rim_rows].add(pass_rim(upper, 1))
    core = core.at[part_rows - rim_rows :].add(pass_rim(lower, -1))
    back = lax.psum_scatter(core, "rep", scatter_dimension=0, tiled=True)
    grad_features = (contract_cols(dz, w_self) + back).astype(jnp.bfloat16)
    return (layer_out, grad_features, grad_self, grad_neigh, grad_bias)


def solution(mesh):
    return jax.shard_map(
        shards,
        mesh=mesh,
        in_specs=(
            P(("dom", "rep"), None),
            P(("dom", "rep")),
            P(("dom", "rep"), None, None, None),
            P(("dom", "rep"), None),
            P(("dom", "rep"), None),
            P(),
            P(),
            P(),
            P(("dom", "rep"), None),
        ),
        out_specs=(P(("dom", "rep"), None), P(("dom", "rep"), None), P(), P(), P()),
        check_vma=False,
    )
```

```python
import jax
import jax.numpy as jnp
from jax import lax
from jax.sharding import PartitionSpec as P

HALO_T = 4


def shifted(value, axis, steps):
    count = lax.axis_size(axis)
    first, last = (max(0, -steps), min(count, count - steps))
    return lax.ppermute(value, axis, [(source, source + steps) for source in range(first, last)])


def with_halo(block, sides, width):
    for axis, dim in sides:
        count = lax.axis_size(axis)
        forward = [(i, i + 1) for i in range(count - 1)]
        backward = [(target, source) for source, target in forward]
        low = lax.ppermute(
            lax.slice_in_dim(block, block.shape[dim] - width, None, axis=dim), axis, forward
        )
        high = lax.ppermute(lax.slice_in_dim(block, 0, width, axis=dim), axis, backward)
        block = jnp.concatenate([low, block, high], axis=dim)
    return block


def contract_rows(left, right):
    return lax.dot_general(
        left, right, (((0,), (0,)), ((), ())), preferred_element_type=jnp.float32
    )


def contract_cols(left, right):
    return lax.dot_general(
        left, right, (((1,), (1,)), ((), ())), preferred_element_type=jnp.float32
    )


HALVING_BITS = (2, 3, 6, 0)
DOUBLING_BITS = (4, 7, 5, 1)


def halving_sum(block, axes):
    count = 1
    for axis in axes:
        count *= lax.axis_size(axis)
    place = lax.axis_index(axes)
    bits = [bit for bit in HALVING_BITS if (1 << bit) < count]
    for bit in bits:
        pairs = [(i, i ^ (1 << bit)) for i in range(count)]
        upper = ((place >> bit) & 1) == 1
        half = block.shape[0] // 2
        kept = jnp.where(upper, block[half:], block[:half])
        sent = jnp.where(upper, block[:half], block[half:])
        block = kept + lax.ppermute(sent, axes, pairs)
    for bit in DOUBLING_BITS:
        if (1 << bit) < count:
            block = block + lax.ppermute(block, axes, [(i, i ^ (1 << bit)) for i in range(count)])
    for bit in reversed(bits):
        pairs = [(i, i ^ (1 << bit)) for i in range(count)]
        upper = ((place >> bit) & 1) == 1
        got = lax.ppermute(block, axes, pairs)
        block = jnp.where(upper, jnp.concatenate([got, block]), jnp.concatenate([block, got]))
    return block


def gather_rep(block):
    count = lax.axis_size("rep")
    place = lax.axis_index("rep")
    if count == 4:
        ahead = [(i, (i + 1) % count) for i in range(count)]
        behind = [(i, (i - 1) % count) for i in range(count)]
        from_prev = lax.ppermute(block, "rep", ahead)
        from_next = lax.ppermute(block, "rep", behind)
        half = block.shape[0] // 2
        far = jnp.concatenate(
            [lax.ppermute(from_prev[:half], "rep", ahead), lax.ppermute(from_next[half:], "rep", behind)]
        )
        parts = [block, from_prev, far, from_next]
    else:
        parts = [block] + [
            lax.ppermute(block, "rep", [(i, (i + shift) % count) for i in range(count)])
            for shift in range(1, count)
        ]
    source = (place - jnp.arange(count)) % count
    return jnp.stack(parts)[source].reshape(count * block.shape[0], *block.shape[1:])


def pass_rim(values, offset):
    return shifted(values.astype(jnp.bfloat16), "dom", offset).astype(values.dtype)


def shards(
    x_loader, owner_index, tile_vals, tile_cols, tile_live, w_self, w_neigh, bias, cotangent
):
    rows, width = x_loader.shape
    reps = lax.axis_size("rep")
    dom_place = lax.axis_index("dom")
    part_rows = rows * reps
    part_tiles = part_rows // 128
    row_tiles = rows // 128
    rim_rows = HALO_T * 128
    dest = owner_index // part_rows
    doms = lax.axis_size("dom")
    per = rows // doms
    line = jnp.arange(rows, dtype=jnp.int32)
    dest_hot = (dest[:, None] == jnp.arange(doms, dtype=jnp.int32)).astype(jnp.bfloat16)
    earlier = (line[:, None] > line[None, :]).astype(jnp.bfloat16)
    before = jnp.dot(earlier, dest_hot, preferred_element_type=jnp.float32)
    rank = jnp.sum(before * dest_hot.astype(jnp.float32), axis=1).astype(jnp.int32)
    to_sorted = ((dest * per + rank)[None, :] == line[:, None]).astype(jnp.bfloat16)
    slot_src = owner_index % rows
    code_src = jnp.stack([slot_src // 32, slot_src % 32], axis=1).astype(jnp.bfloat16)
    code = jnp.dot(to_sorted, code_src, preferred_element_type=jnp.float32)
    code = jnp.concatenate([code[:, 0].reshape(doms, per), code[:, 1].reshape(doms, per)], axis=1)
    code = jnp.pad(code.astype(jnp.bfloat16), ((0, 0), (0, 128 - 2 * per)))
    x_sorted = jnp.dot(to_sorted, x_loader, preferred_element_type=jnp.float32).astype(jnp.bfloat16)
    sent = jnp.concatenate([x_sorted.reshape(doms, per * width), code], axis=1)
    got = lax.all_to_all(sent, "dom", split_axis=0, concat_axis=0, tiled=True)
    moved = got[:, : per * width].reshape(rows, width)
    codes = got[:, per * width : per * width + 2 * per].astype(jnp.int32)
    slot = (codes[:, :per] * 32 + codes[:, per:]).reshape(rows)
    to_owner = (slot[None, :] == line[:, None]).astype(jnp.bfloat16)
    features = jnp.dot(to_owner, moved, preferred_element_type=jnp.float32).astype(jnp.bfloat16)
    first_tile = dom_place * part_tiles - HALO_T
    local_cols = tile_cols - first_tile
    masked = tile_vals * tile_live.astype(jnp.bfloat16)[:, :, None, None]
    degree = 1.0 + jnp.sum(masked, axis=(1, 3), dtype=jnp.float32)
    whole = gather_rep(features)
    extended = with_halo(whole, (("dom", 0),), rim_rows)
    span_tiles = part_tiles + 2 * HALO_T
    onehot = (local_cols[:, :, None] == jnp.arange(span_tiles, dtype=jnp.int32)).astype(jnp.bfloat16)
    merged = jnp.einsum("tke,tkab->teab", onehot, masked, preferred_element_type=jnp.float32)
    merged_hi = merged.astype(jnp.bfloat16)
    merged_lo = (merged - merged_hi.astype(jnp.float32)).astype(jnp.bfloat16)
    span = extended.reshape(span_tiles, 128, width)
    summed = jnp.einsum(
        "teab,ebf->taf", merged_hi, span, preferred_element_type=jnp.float32
    ) + jnp.einsum("teab,ebf->taf", merged_lo, span, preferred_element_type=jnp.float32)
    agg = (summed / degree[:, :, None]).reshape(rows, width).astype(jnp.bfloat16)
    pre = (
        jnp.dot(features, w_self, preferred_element_type=jnp.float32)
        + jnp.dot(agg, w_neigh, preferred_element_type=jnp.float32)
        + bias
    )
    layer_out = jnp.where(pre > 0, pre, jnp.expm1(jnp.minimum(pre, 0.0))).astype(jnp.bfloat16)
    slope = jnp.where(pre > 0, 1.0, jnp.exp(jnp.minimum(pre, 0.0)))
    dz = (cotangent.astype(jnp.float32) * slope).astype(jnp.bfloat16)
    lanes = 2 * width * width // 256
    packed = halving_sum(
        jnp.concatenate(
            [
                jnp.concatenate([contract_rows(features, dz), contract_rows(agg, dz)]).reshape(256, lanes),
                jnp.pad(jnp.sum(dz, axis=0, dtype=jnp.float32).reshape(256, -1), ((0, 0), (0, 126))),
            ],
            axis=1,
        ),
        ("dom", "rep"),
    )
    grads = packed[:, :lanes].reshape(2 * width, width)
    grad_self, grad_neigh = grads[:width], grads[width:]
    grad_bias = packed[:, lanes : lanes + 2].reshape(width)
    scaled = (contract_cols(dz, w_neigh) / degree.reshape(rows, 1)).astype(jnp.bfloat16)
    scaled_tiles = scaled.reshape(row_tiles, 128, width)
    buffer = jnp.einsum(
        "teab,taf->ebf", merged_hi, scaled_tiles, preferred_element_type=jnp.float32
    ) + jnp.einsum("teab,taf->ebf", merged_lo, scaled_tiles, preferred_element_type=jnp.float32)
    buffer = buffer.reshape(span_tiles * 128, width)
    lower = buffer[:rim_rows]
    upper = buffer[rim_rows + part_rows :]
    core = buffer[rim_rows : rim_rows + part_rows]
    core = core.at[:rim_rows].add(pass_rim(upper, 1))
    core = core.at[part_rows - rim_rows :].add(pass_rim(lower, -1))
    back = lax.psum_scatter(core, "rep", scatter_dimension=0, tiled=True)
    grad_features = (contract_cols(dz, w_self) + back).astype(jnp.bfloat16)
    return (layer_out, grad_features, grad_self, grad_neigh, grad_bias)


def solution(mesh):
    return jax.shard_map(
        shards,
        mesh=mesh,
        in_specs=(
            P(("dom", "rep"), None),
            P(("dom", "rep")),
            P(("dom", "rep"), None, None, None),
            P(("dom", "rep"), None),
            P(("dom", "rep"), None),
            P(),
            P(),
            P(),
            P(("dom", "rep"), None),
        ),
        out_specs=(P(("dom", "rep"), None), P(("dom", "rep"), None), P(), P(), P()),
        check_vma=False,
    )
```

```python
import jax
import jax.numpy as jnp
from jax import lax
from jax.sharding import PartitionSpec as P

HALO_T = 4


def shifted(value, axis, steps):
    count = lax.axis_size(axis)
    first, last = (max(0, -steps), min(count, count - steps))
    return lax.ppermute(value, axis, [(source, source + steps) for source in range(first, last)])


def with_halo(block, sides, width):
    for axis, dim in sides:
        count = lax.axis_size(axis)
        forward = [(i, i + 1) for i in range(count - 1)]
        backward = [(target, source) for source, target in forward]
        low = lax.ppermute(
            lax.slice_in_dim(block, block.shape[dim] - width, None, axis=dim), axis, forward
        )
        high = lax.ppermute(lax.slice_in_dim(block, 0, width, axis=dim), axis, backward)
        block = jnp.concatenate([low, block, high], axis=dim)
    return block


def contract_rows(left, right):
    return lax.dot_general(
        left, right, (((0,), (0,)), ((), ())), preferred_element_type=jnp.float32
    )


def contract_cols(left, right):
    return lax.dot_general(
        left, right, (((1,), (1,)), ((), ())), preferred_element_type=jnp.float32
    )


HALVING_BITS = (2, 3, 6, 0)
DOUBLING_BITS = (4, 7, 5, 1)


def halving_sum(block, axes):
    count = 1
    for axis in axes:
        count *= lax.axis_size(axis)
    place = lax.axis_index(axes)
    bits = [bit for bit in HALVING_BITS if (1 << bit) < count]
    for bit in bits:
        pairs = [(i, i ^ (1 << bit)) for i in range(count)]
        upper = ((place >> bit) & 1) == 1
        half = block.shape[0] // 2
        kept = jnp.where(upper, block[half:], block[:half])
        sent = jnp.where(upper, block[:half], block[half:])
        block = kept + lax.ppermute(sent, axes, pairs)
    for bit in DOUBLING_BITS:
        if (1 << bit) < count:
            block = block + lax.ppermute(block, axes, [(i, i ^ (1 << bit)) for i in range(count)])
    for bit in reversed(bits):
        pairs = [(i, i ^ (1 << bit)) for i in range(count)]
        upper = ((place >> bit) & 1) == 1
        got = lax.ppermute(block, axes, pairs)
        block = jnp.where(upper, jnp.concatenate([got, block]), jnp.concatenate([block, got]))
    return block


def gather_rep(block):
    count = lax.axis_size("rep")
    place = lax.axis_index("rep")
    if count == 4:
        ahead = [(i, (i + 1) % count) for i in range(count)]
        behind = [(i, (i - 1) % count) for i in range(count)]
        from_prev = lax.ppermute(block, "rep", ahead)
        from_next = lax.ppermute(block, "rep", behind)
        half = block.shape[0] // 2
        far = jnp.concatenate(
            [lax.ppermute(from_prev[:half], "rep", ahead), lax.ppermute(from_next[half:], "rep", behind)]
        )
        parts = [block, from_prev, far, from_next]
    else:
        parts = [block] + [
            lax.ppermute(block, "rep", [(i, (i + shift) % count) for i in range(count)])
            for shift in range(1, count)
        ]
    rows = block.shape[0]
    whole = jnp.zeros((count * rows, *block.shape[1:]), block.dtype)
    for shift, part in enumerate(parts):
        whole = lax.dynamic_update_slice_in_dim(whole, part, ((place - shift) % count) * rows, axis=0)
    return whole


def pass_rim(values, offset):
    return shifted(values.astype(jnp.bfloat16), "dom", offset).astype(values.dtype)


def shards(
    x_loader, owner_index, tile_vals, tile_cols, tile_live, w_self, w_neigh, bias, cotangent
):
    rows, width = x_loader.shape
    reps = lax.axis_size("rep")
    dom_place = lax.axis_index("dom")
    part_rows = rows * reps
    part_tiles = part_rows // 128
    row_tiles = rows // 128
    rim_rows = HALO_T * 128
    dest = owner_index // part_rows
    doms = lax.axis_size("dom")
    per = rows // doms
    line = jnp.arange(rows, dtype=jnp.int32)
    dest_hot = (dest[:, None] == jnp.arange(doms, dtype=jnp.int32)).astype(jnp.bfloat16)
    earlier = (line[:, None] > line[None, :]).astype(jnp.bfloat16)
    before = jnp.dot(earlier, dest_hot, preferred_element_type=jnp.float32)
    rank = jnp.sum(before * dest_hot.astype(jnp.float32), axis=1).astype(jnp.int32)
    to_sorted = ((dest * per + rank)[None, :] == line[:, None]).astype(jnp.bfloat16)
    slot_src = owner_index % rows
    code_src = jnp.stack([slot_src // 32, slot_src % 32], axis=1).astype(jnp.bfloat16)
    code = jnp.dot(to_sorted, code_src, preferred_element_type=jnp.float32)
    code = jnp.concatenate([code[:, 0].reshape(doms, per), code[:, 1].reshape(doms, per)], axis=1)
    code = jnp.pad(code.astype(jnp.bfloat16), ((0, 0), (0, 128 - 2 * per)))
    x_sorted = jnp.dot(to_sorted, x_loader, preferred_element_type=jnp.float32).astype(jnp.bfloat16)
    sent = jnp.concatenate([x_sorted.reshape(doms, per * width), code], axis=1)
    got = lax.all_to_all(sent, "dom", split_axis=0, concat_axis=0, tiled=True)
    moved = got[:, : per * width].reshape(rows, width)
    codes = got[:, per * width : per * width + 2 * per].astype(jnp.int32)
    slot = (codes[:, :per] * 32 + codes[:, per:]).reshape(rows)
    to_owner = (slot[None, :] == line[:, None]).astype(jnp.bfloat16)
    features = jnp.dot(to_owner, moved, preferred_element_type=jnp.float32).astype(jnp.bfloat16)
    first_tile = dom_place * part_tiles - HALO_T
    local_cols = tile_cols - first_tile
    masked = tile_vals * tile_live.astype(jnp.bfloat16)[:, :, None, None]
    degree = 1.0 + jnp.sum(masked, axis=(1, 3), dtype=jnp.float32)
    whole = gather_rep(features)
    extended = with_halo(whole, (("dom", 0),), rim_rows)
    span_tiles = part_tiles + 2 * HALO_T
    onehot = (local_cols[:, :, None] == jnp.arange(span_tiles, dtype=jnp.int32)).astype(jnp.bfloat16)
    merged = jnp.einsum("tke,tkab->teab", onehot, masked, preferred_element_type=jnp.float32)
    merged_hi = merged.astype(jnp.bfloat16)
    merged_lo = (merged - merged_hi.astype(jnp.float32)).astype(jnp.bfloat16)
    span = extended.reshape(span_tiles, 128, width)
    summed = jnp.einsum(
        "teab,ebf->taf", merged_hi, span, preferred_element_type=jnp.float32
    ) + jnp.einsum("teab,ebf->taf", merged_lo, span, preferred_element_type=jnp.float32)
    agg = (summed / degree[:, :, None]).reshape(rows, width).astype(jnp.bfloat16)
    pre = (
        jnp.dot(features, w_self, preferred_element_type=jnp.float32)
        + jnp.dot(agg, w_neigh, preferred_element_type=jnp.float32)
        + bias
    )
    layer_out = jnp.where(pre > 0, pre, jnp.expm1(jnp.minimum(pre, 0.0))).astype(jnp.bfloat16)
    slope = jnp.where(pre > 0, 1.0, jnp.exp(jnp.minimum(pre, 0.0)))
    dz = (cotangent.astype(jnp.float32) * slope).astype(jnp.bfloat16)
    lanes = 2 * width * width // 256
    packed = halving_sum(
        jnp.concatenate(
            [
                jnp.concatenate([contract_rows(features, dz), contract_rows(agg, dz)]).reshape(256, lanes),
                jnp.pad(jnp.sum(dz, axis=0, dtype=jnp.float32).reshape(256, -1), ((0, 0), (0, 126))),
            ],
            axis=1,
        ),
        ("dom", "rep"),
    )
    grads = packed[:, :lanes].reshape(2 * width, width)
    grad_self, grad_neigh = grads[:width], grads[width:]
    grad_bias = packed[:, lanes : lanes + 2].reshape(width)
    scaled = (contract_cols(dz, w_neigh) / degree.reshape(rows, 1)).astype(jnp.bfloat16)
    scaled_tiles = scaled.reshape(row_tiles, 128, width)
    buffer = jnp.einsum(
        "teab,taf->ebf", merged_hi, scaled_tiles, preferred_element_type=jnp.float32
    ) + jnp.einsum("teab,taf->ebf", merged_lo, scaled_tiles, preferred_element_type=jnp.float32)
    buffer = buffer.reshape(span_tiles * 128, width)
    lower = buffer[:rim_rows]
    upper = buffer[rim_rows + part_rows :]
    core = buffer[rim_rows : rim_rows + part_rows]
    core = core.at[:rim_rows].add(pass_rim(upper, 1))
    core = core.at[part_rows - rim_rows :].add(pass_rim(lower, -1))
    back = lax.psum_scatter(core, "rep", scatter_dimension=0, tiled=True)
    grad_features = (contract_cols(dz, w_self) + back).astype(jnp.bfloat16)
    return (layer_out, grad_features, grad_self, grad_neigh, grad_bias)


def solution(mesh):
    return jax.shard_map(
        shards,
        mesh=mesh,
        in_specs=(
            P(("dom", "rep"), None),
            P(("dom", "rep")),
            P(("dom", "rep"), None, None, None),
            P(("dom", "rep"), None),
            P(("dom", "rep"), None),
            P(),
            P(),
            P(),
            P(("dom", "rep"), None),
        ),
        out_specs=(P(("dom", "rep"), None), P(("dom", "rep"), None), P(), P(), P()),
        check_vma=False,
    )
```
